256 devices in a mesh: seq: 32 (over y, x, z_lo), tensor: 8 (over z_hi, core).
Axes of the slice: x: 4, y: 4, z: 8 (z_hi: 4, z_lo: 2; z = z_hi * 2 + z_lo), core: 2. Of those that a mesh axis runs over, the one named last changes fastest.
Arguments:
- residual: bfloat16 [4096, 2048], P('seq', 'tensor'), may hold values from -10 to 10
- queries: bfloat16 [4096, 2048], P('seq', 'tensor'), may hold values from -5 to 5
- new_keys: bfloat16 [4096, 2048], P('seq', 'tensor'), may hold values from -5 to 5
- new_values: bfloat16 [4096, 2048], P('seq', 'tensor'), may hold values from -6 to 6
- cache_keys: bfloat16 [8, 16384, 2048], P(None, 'seq', 'tensor'), may hold values from -5 to 5
- cache_values: bfloat16 [8, 16384, 2048], P(None, 'seq', 'tensor'), may hold values from -6 to 6
- cache_lengths: int32 [8], replicated, may hold values from 1 to 16384, 23552 in all
- out_proj: bfloat16 [2048, 2048], P('tensor'), may hold values from -0.125 to 0.125
- norm_gain: float32 [2048], P('tensor'), may hold values from 0.5 to 1.5
- router: bfloat16 [2048, 64], P('tensor'), may hold values from -0.3984375 to 0.3984375
- expert_ids: int32 [4096, 6], P('seq'), may hold values from 0 to 63, all different within a row; in each aligned block of 128 rows (0 to 127, 128 to 255, ...) at most 16 rows name the same one
- expert_gate_up: bfloat16 [64, 2048, 2, 1408], P('seq', None, None, 'tensor'), may hold values from -0.125 to 0.125
- expert_down: bfloat16 [64, 1408, 2048], P('seq', 'tensor'), may hold values from -0.15625 to 0.15625
- shared_gate_up: bfloat16 [2048, 2, 1408], P(None, None, 'tensor'), may hold values from -0.125 to 0.125
- shared_down: bfloat16 [1408, 2048], P('tensor'), may hold values from -0.15625 to 0.15625
Outputs:
- layer_out: bfloat16 [4096, 2048], P('seq', 'tensor')
The draws below stay inside these ranges and needn't reach their ends.
Inputs may be any that keep to these rules, and one draw needn't show every extreme that they name: Request r's cached tokens are positions 0 to cache_lengths[r] - 1 of its row of 16384 cache positions; the lengths sum to 16384 + 7 * (1024) and the longest equals 16384. `expert_ids`: each row names 6 different experts. Among the 128 rows of one index of seq no expert is named by more than 16 rows, and this bound is reached.
All inputs are finite; a program needn't handle non-finite values.
Results may differ from the reference program's by a relative error of at most 0.025.
Values may be sent and summed in bfloat16 or wider, within the bound.
No kernel may reach another device: no remote copies, remote signals or barrier semaphores. Data moves between devices by JAX's collectives and lax.ppermute only.
A program may use at most 128 MiB of HBM per device.

```python
import math
import jax
import jax.numpy as jnp
import numpy as np
from jax import lax

D = 2048
HEADS = 16
HD = 128
FFE = 1408
SHF = 1408
TOPK = 6
NEW = 512
TOK_DEV = 128
CLEN_DEV = 512
TOKENS = 4096
REQS = 8
CLEN = 16384
EXPERTS = 64
CAP = 16
N_SEQ = 32
N_TENSOR = 8


def sign_table(key):
    flips = jax.random.bernoulli(jax.random.fold_in(key, 101), 0.5, (REQS, HEADS * HD))
    return jnp.where(flips, 1.0, -1.0).astype(jnp.float32)


def planted_levels():
    places = lax.iota(jnp.int32, NEW)
    levels = 3.5 + 0.5 * places.astype(jnp.float32)
    return jnp.where((places >= 1) & (places <= 3), levels, 0.0)


def draw_residual(key, part):
    columns = lax.iota(jnp.float32, D) / D
    spread = jnp.power(10.0, jax.random.uniform(jax.random.fold_in(key, 11), (D,), jnp.float32))
    noise = jnp.clip(jax.random.normal(jax.random.fold_in(key, 12), (TOKENS, D), jnp.float32), -4.0, 4.0)
    values = 0.02 * jnp.power(3.0, columns) * spread * noise
    return values.astype(jnp.bfloat16)


def draw_queries(key, part):
    width = HEADS * HD
    noise = jnp.clip(jax.random.normal(jax.random.fold_in(key, 21), (REQS, NEW, width), jnp.float32), -4.0, 4.0)
    levels = planted_levels()
    planted = levels[None, :, None] * sign_table(key)[:, None, :]
    values = jnp.where(levels[None, :, None] > 0.0, planted, noise)
    return values.reshape(TOKENS, width).astype(jnp.bfloat16)


def draw_cache_keys(key, part):
    width = HEADS * HD
    noise = jnp.clip(1.25 * jax.random.normal(jax.random.fold_in(key, 31), (REQS, CLEN, width), jnp.float32), -5.0, 5.0)
    first = (lax.iota(jnp.int32, CLEN) == 0)[None, :, None]
    values = jnp.where(first, 5.0 * sign_table(key)[:, None, :], noise)
    return values.astype(jnp.bfloat16)


def draw_new_keys(key, part):
    width = HEADS * HD
    noise = jnp.clip(1.25 * jax.random.normal(jax.random.fold_in(key, 41), (REQS, NEW, width), jnp.float32), -5.0, 5.0)
    first = (lax.iota(jnp.int32, NEW) == 0)[None, :, None]
    values = jnp.where(first, 4.9375 * sign_table(key)[:, None, :], noise)
    return values.reshape(TOKENS, width).astype(jnp.bfloat16)


def block_scale(rng, dims, cuts, smallest, largest):
    level, own = 1.0, jax.random.fold_in(rng, 6)
    for dim, shards_of in cuts:
        heights = jnp.exp(jax.random.uniform(jax.random.fold_in(own, dim), (shards_of,), jnp.float32, smallest / len(cuts), largest / len(cuts)))
        level = level * jnp.repeat(heights, dims[dim] // shards_of).reshape([-1 if axis == dim else 1 for axis in range(len(dims))])
    return level


def profile(number_of, total, most, slope):
    portions = [(1 << 20) // math.isqrt(standing ** slope) + 1 for standing in range(2, number_of + 1)]
    rest, holding = total - most - (number_of - 1), [1] * (number_of - 1)
    while rest > 0:
        candidates = [i for i in range(number_of - 1) if holding[i] < most]
        mass, remaining = sum([portions[i] for i in candidates]), rest
        for i in candidates:
            addition = min(most - holding[i], max(1, remaining * portions[i] // mass), rest)
            holding[i] = holding[i] + addition
            rest = rest - addition
    return np.array([most] + holding)


def uneven_parts(own_key, count, total, limit, lean):
    if count == 2:
        one = jax.random.randint(own_key, (), max(1, total - limit), min(limit, total - 1) + 1)
        return jnp.stack([one, total - one])
    sizes = jnp.asarray(profile(count, total, limit, lean), jnp.int32)
    couples = (count - 1) // 2
    source_of, taker = sizes[1:1 + 2 * couples:2], sizes[2:2 + 2 * couples:2]
    slack = jnp.minimum(source_of - 1, limit - taker)
    moved = jax.random.randint(jax.random.fold_in(own_key, 1), (couples,), 0, 1 << 20) % (slack + 1)
    sizes = sizes.at[1:1 + 2 * couples:2].set(source_of - moved).at[2:2 + 2 * couples:2].set(taker + moved)
    return sizes[jax.random.permutation(jax.random.fold_in(own_key, 2), count)]


def routed_block(key, own, number, rows, number_of, top, reach, slope):
    ranking = jax.random.permutation(key, number_of)
    packed, common = shares(number_of, rows * top, reach, slope, True), shares(number_of, rows * top, reach, slope, False)
    places = jnp.arange(number_of)

    def named(tallies, offset_by):
        used = int((tallies > 0).sum())
        fixed = max(1, used // 4)
        moved = fixed + (places - fixed + offset_by * (used - fixed)) % max(1, number_of - fixed)
        return jnp.zeros((number_of,), jnp.int32).at[ranking[jnp.where(places < fixed, places, moved)]].set(jnp.asarray(tallies, jnp.int32))

    tallies = jnp.where(number % 4 == 0, named(packed, number // 4), named(common, number - number // 4 - 1))
    mixed = jax.random.permutation(jax.random.fold_in(own, 3), number_of)
    source_of, receiver = mixed[0:number_of // 2 * 2:2], mixed[1:number_of // 2 * 2:2]
    margin = jnp.minimum(tallies[source_of] - 1, reach - tallies[receiver]) // 2
    margin = jnp.where((source_of == ranking[0]) | (receiver == ranking[0]) | (tallies[receiver] == 0), 0, jnp.maximum(margin, 0))
    moved = jax.random.randint(jax.random.fold_in(own, 4), (number_of // 2,), 0, 1 << 20) % (margin + 1)
    tallies = tallies.at[source_of].add(-moved).at[receiver].add(moved)
    labels = jnp.searchsorted(jnp.cumsum(tallies), jnp.arange(rows * top), side="right").astype(jnp.int32)
    grid = labels.reshape(top, rows).T
    grid = grid[jax.random.permutation(jax.random.fold_in(own, 1), rows)]
    offset_by = jax.random.randint(jax.random.fold_in(own, 2), (rows, 1), 0, top)
    return jnp.take_along_axis(grid, (jnp.arange(top)[None, :] + offset_by) % top, axis=1)


def shares(amount, total, bound, lean, full):
    weights = [(1 << 20) // math.isqrt(grade ** lean) + 1 for grade in range(1, amount + 1)]
    largest = bound if full else min(bound, max(-(-total // amount), total * weights[0] // sum(weights)))
    least = 1 if total - largest >= amount - 1 else 0
    holding, rest = [largest] + [least] * (amount - 1), total - largest - least * (amount - 1)
    while rest > 0:
        candidates = [i for i in range(1, amount) if holding[i] < largest] or [i for i in range(1, amount) if holding[i] < bound]
        pool, budget = sum([weights[i] for i in candidates]), rest
        for i in candidates:
            extra = min(bound - holding[i], max(1, budget * weights[i] // pool), rest)
            holding[i] = holding[i] + extra
            rest = rest - extra
    return np.array(holding)


def scatter_about(key, dims, scale, reach, pieces=(), kind=jnp.bfloat16):
    array = jax.random.normal(key, dims, jnp.float32) * scale
    if len(pieces) > 0:
        array = block_scale(key, dims, pieces, -0.22, 0.18) * array
    return jnp.clip(array, min=-reach, max=reach).astype(kind)


def setup_inputs(seed: int = 0) -> dict:
    streams_of = jax.random.split(jax.random.key(seed), 16)
    residual = draw_residual(jax.random.fold_in(streams_of[15], 71), 0)
    queries = draw_queries(jax.random.fold_in(streams_of[15], 71), 0)
    new_keys = draw_new_keys(jax.random.fold_in(streams_of[15], 71), 0)
    new_values = scatter_about(streams_of[3], (TOKENS, HEADS * HD), 1.0, 6.0, ((0, 32), (1, 8)))
    cache_keys = draw_cache_keys(jax.random.fold_in(streams_of[15], 71), 0)
    cache_values = scatter_about(streams_of[5], (REQS, CLEN, HEADS * HD), 1.0, 6.0, ((1, 32), (2, 8)))
    cache_lengths = uneven_parts(streams_of[6], REQS, CLEN + (REQS - 1) * (CLEN // 16), CLEN, 2).astype(jnp.int32)
    out_proj = scatter_about(streams_of[7], (HEADS * HD, D), (HEADS * HD) ** -0.5, 0.125, ((0, 8),))
    norm_gain = jnp.clip(1.0 + 0.1 * jax.random.normal(streams_of[8], (D,), jnp.float32), 0.5, 1.5)
    router = scatter_about(streams_of[9], (D, EXPERTS), 0.066, 0.3984375, ((0, 8),))
    expert_ids_keys = jax.random.split(jax.random.fold_in(streams_of[10], 1), TOKENS // TOK_DEV)
    expert_ids_turns = jax.random.permutation(jax.random.fold_in(streams_of[10], 3), TOKENS // TOK_DEV)
    expert_ids = jax.vmap(lambda own, number: routed_block(jax.random.fold_in(streams_of[10], 2), own, number, TOK_DEV, EXPERTS, TOPK, CAP, 2))(expert_ids_keys, expert_ids_turns).reshape((TOKENS, TOPK))
    expert_gate_up = scatter_about(streams_of[11], (EXPERTS, D, 2, FFE), D ** -0.5, 0.125, ((0, 32), (3, 8)))
    expert_down = scatter_about(streams_of[12], (EXPERTS, FFE, D), FFE ** -0.5, 0.15625, ((0, 32), (1, 8)))
    shared_gate_up = scatter_about(streams_of[13], (D, 2, SHF), D ** -0.5, 0.125, ((2, 8),))
    shared_down = scatter_about(streams_of[14], (SHF, D), SHF ** -0.5, 0.15625, ((0, 8),))
    return {"residual": residual, "queries": queries, "new_keys": new_keys, "new_values": new_values, "cache_keys": cache_keys, "cache_values": cache_values, "cache_lengths": cache_lengths, "out_proj": out_proj, "norm_gain": norm_gain, "router": router, "expert_ids": expert_ids, "expert_gate_up": expert_gate_up, "expert_down": expert_down, "shared_gate_up": shared_gate_up, "shared_down": shared_down}


negative = -1e+30
epsilon = 1e-06

def block_partial(scores, visible, values):
    masked = jnp.where(visible, scores, negative)
    block_max = lax.optimization_barrier(jnp.max(masked, -1))
    shifted = jnp.where(visible, scores, block_max[..., None]) - block_max[..., None]
    weights = jnp.where(visible, jnp.exp(shifted), 0.0)
    block_sum = lax.optimization_barrier(jnp.sum(weights, -1))
    rounded = lax.optimization_barrier(weights.astype(jnp.bfloat16)).astype(jnp.float32)
    block_out = jnp.einsum('hqbk,bkhd->hqbd', rounded, values.astype(jnp.float32))
    return (block_max, block_sum, block_out)

def one_request(request):
    query_rows, keys_cached, values_cached, keys_new, values_new, length = request
    scaling = 1.0 / math.sqrt(HD)
    queries_wide = query_rows.astype(jnp.float32)
    new_blocks = NEW // TOK_DEV
    cached_scores = jnp.einsum('qhd,khd->hqk', queries_wide, keys_cached.astype(jnp.float32)) * scaling
    cached_scores = cached_scores.reshape(HEADS, NEW, N_SEQ, CLEN_DEV)
    visible_cached = (lax.iota(jnp.int32, CLEN) < length.astype(jnp.int32)).reshape(1, 1, N_SEQ, CLEN_DEV)
    max_cached, sum_cached, out_cached = block_partial(cached_scores, visible_cached, values_cached.reshape(N_SEQ, CLEN_DEV, HEADS, HD))
    new_scores = jnp.einsum('qhd,khd->hqk', queries_wide, keys_new.astype(jnp.float32)) * scaling
    new_scores = new_scores.reshape(HEADS, NEW, new_blocks, TOK_DEV)
    places = lax.iota(jnp.int32, NEW)
    visible_new = (places[:, None] >= places[None, :]).reshape(1, NEW, new_blocks, TOK_DEV)
    max_new, sum_new, out_new = block_partial(new_scores, visible_new, values_new.reshape(new_blocks, TOK_DEV, HEADS, HD))
    block_max = jnp.concatenate([max_cached, max_new], -1)
    block_sum = jnp.concatenate([sum_cached, sum_new], -1)
    block_out = jnp.concatenate([out_cached, out_new], 2)
    row_max = lax.optimization_barrier(jnp.max(block_max, -1))
    factors = jnp.exp(block_max - row_max[..., None])
    row_sum = lax.optimization_barrier(jnp.sum(block_sum * factors, -1))
    weighted = lax.optimization_barrier(jnp.sum(block_out * factors[..., None], 2))
    attended = (weighted / row_sum[..., None]).astype(jnp.bfloat16)
    return jnp.transpose(attended, (1, 0, 2)).reshape(NEW, HEADS * HD)

def routed_outputs(normed, expert_ids, expert_gate_up, expert_down):
    flat_ids = expert_ids.reshape(-1).astype(jnp.int32)
    count = flat_ids.shape[0]
    padded = jnp.concatenate([normed, jnp.zeros((1, D), normed.dtype)], 0)
    most_rows = N_SEQ * CAP
    group = FFE // N_TENSOR

    def one_expert(expert, result):
        places = jnp.nonzero(flat_ids == expert, size=most_rows, fill_value=count)[0].astype(jnp.int32)
        rows = padded[(places // TOPK).astype(jnp.int32)].astype(jnp.float32)
        gate_up = expert_gate_up[expert].astype(jnp.float32).reshape(D, 2, N_TENSOR, group)
        pair = jnp.einsum('md,dcjg->mcjg', rows, gate_up)
        hidden_act = (jax.nn.silu(pair[:, 0]) * pair[:, 1]).astype(jnp.bfloat16)
        down = expert_down[expert].astype(jnp.float32).reshape(N_TENSOR, group, D)
        parts = jnp.einsum('mjg,jgd->mjd', hidden_act.astype(jnp.float32), down).astype(jnp.bfloat16)
        outputs = lax.optimization_barrier(jnp.sum(parts.astype(jnp.float32), 1)).astype(jnp.bfloat16)
        return result.at[places].set(outputs, mode='drop')
    result = lax.fori_loop(0, EXPERTS, one_expert, jnp.zeros((count, D), jnp.bfloat16))
    return result.reshape(TOKENS, TOPK, D)

def reference(residual, queries, new_keys, new_values, cache_keys, cache_values, cache_lengths, out_proj, norm_gain, router, expert_ids, expert_gate_up, expert_down, shared_gate_up, shared_down):
    requests = (queries.reshape(REQS, NEW, HEADS, HD), cache_keys.reshape(REQS, CLEN, HEADS, HD), cache_values.reshape(REQS, CLEN, HEADS, HD), new_keys.reshape(REQS, NEW, HEADS, HD), new_values.reshape(REQS, NEW, HEADS, HD), cache_lengths.astype(jnp.int32))
    attended = lax.map(one_request, requests).reshape(TOKENS, HEADS * HD)
    attn_out = jnp.dot(attended, out_proj, preferred_element_type=jnp.float32)
    stream = residual.astype(jnp.float32) + attn_out
    inverse_rms = lax.rsqrt(lax.optimization_barrier(jnp.mean(stream * stream, 1)) + epsilon)
    normed = (stream * inverse_rms[:, None] * norm_gain).astype(jnp.bfloat16)
    logits = jnp.dot(normed, router, preferred_element_type=jnp.float32)
    chosen = jax.nn.sigmoid(jnp.take_along_axis(logits, expert_ids.astype(jnp.int32), 1))
    gates = chosen / lax.optimization_barrier(jnp.sum(chosen, 1, keepdims=True))
    pair = jnp.einsum('td,dcf->tcf', normed.astype(jnp.float32), shared_gate_up.astype(jnp.float32))
    shared_act = (jax.nn.silu(pair[:, 0]) * pair[:, 1]).astype(jnp.bfloat16)
    shared_out = jnp.dot(shared_act, shared_down, preferred_element_type=jnp.float32)
    routed = routed_outputs(normed, expert_ids, expert_gate_up, expert_down)
    mixture = lax.optimization_barrier(jnp.sum(gates[..., None] * routed.astype(jnp.float32), 1))
    return (stream + shared_out + mixture).astype(jnp.bfloat16)
```

```python
import math

import jax
import jax.numpy as jnp
from jax import lax
from jax.sharding import PartitionSpec as P

D = 2048
HD = 128
NEW = 512


negative = -1e30
epsilon = 1e-06


def block_partial(scores, visible, values):
    masked = jnp.where(visible, scores, negative)
    block_max = jnp.max(masked, -1)
    shifted = jnp.where(visible, scores, block_max[..., None]) - block_max[..., None]
    weights = jnp.where(visible, jnp.exp(shifted), 0.0)
    block_sum = jnp.sum(weights, -1)
    block_out = jnp.einsum(
        "hqk,khd->qhd", weights.astype(jnp.bfloat16), values, preferred_element_type=jnp.float32
    )
    return (block_max, block_sum, block_out)


def shards(
    residual,
    queries,
    new_keys,
    new_values,
    cache_keys,
    cache_values,
    cache_lengths,
    out_proj,
    norm_gain,
    router,
    expert_ids,
    expert_gate_up,
    expert_down,
    shared_gate_up,
    shared_down,
):
    seq_count = lax.axis_size("seq")
    tensor_count = lax.axis_size("tensor")
    seq_index = lax.axis_index("seq")
    tok_dev = queries.shape[0]
    heads_local = queries.shape[1] // HD
    requests = tok_dev * seq_count // NEW
    clen_dev = cache_keys.shape[1]
    tokens = tok_dev * seq_count
    width_local = residual.shape[1]
    experts = router.shape[1]
    exp_dev = expert_gate_up.shape[0]
    topk = expert_ids.shape[1]
    scaling = 1.0 / math.sqrt(HD)
    spread = jnp.broadcast_to(queries[None], (seq_count,) + queries.shape)
    every_query = lax.all_to_all(spread, "seq", 0, 0, tiled=True).reshape(tokens, width_local)
    grouped = every_query.reshape(requests, NEW, heads_local, HD)
    first_place = seq_index * clen_dev

    def cached_part(request):
        query_block, key_block, value_block, length = request
        scores = (
            jnp.einsum("qhd,khd->hqk", query_block, key_block, preferred_element_type=jnp.float32)
            * scaling
        )
        visible = (first_place + lax.iota(jnp.int32, clen_dev) < length)[None, None, :]
        return block_partial(scores, visible, value_block)

    max_cached, sum_cached, out_cached = lax.map(
        cached_part,
        (
            grouped,
            cache_keys.reshape(requests, clen_dev, heads_local, HD),
            cache_values.reshape(requests, clen_dev, heads_local, HD),
            cache_lengths,
        ),
    )
    max_cached = jnp.transpose(max_cached, (0, 2, 1))
    sum_cached = jnp.transpose(sum_cached, (0, 2, 1))
    own_start = seq_index * tok_dev
    own_request = own_start // NEW
    offset = own_start % NEW
    own_queries = lax.dynamic_index_in_dim(grouped, own_request, 0, keepdims=False)
    new_scores = (
        jnp.einsum(
            "qhd,khd->hqk",
            own_queries,
            new_keys.reshape(tok_dev, heads_local, HD),
            preferred_element_type=jnp.float32,
        )
        * scaling
    )
    visible_new = (
        lax.iota(jnp.int32, NEW)[:, None] >= offset + lax.iota(jnp.int32, tok_dev)[None, :]
    )[None]
    max_new, sum_new, out_new = block_partial(
        new_scores, visible_new, new_values.reshape(tok_dev, heads_local, HD)
    )
    chosen_request = (lax.iota(jnp.int32, requests) == own_request)[:, None, None]
    max_placed = jnp.where(chosen_request, jnp.transpose(max_new)[None], negative)
    sum_placed = jnp.where(chosen_request, jnp.transpose(sum_new)[None], 0.0)
    out_placed = jnp.where(chosen_request[..., None], out_new[None], 0.0)
    local_max = jnp.maximum(max_cached, max_placed)
    factor_cached = jnp.exp(max_cached - local_max)
    factor_new = jnp.exp(max_placed - local_max)
    local_sum = sum_cached * factor_cached + sum_placed * factor_new
    local_out = out_cached * factor_cached[..., None] + out_placed * factor_new[..., None]
    flat_max = local_max.reshape(seq_count, tok_dev, heads_local)
    flat_sum = local_sum.reshape(seq_count, tok_dev, heads_local)
    stats = lax.all_to_all(
        jnp.stack([flat_max, flat_sum], -1), "seq", 0, 0, tiled=True
    )
    parts_out = lax.all_to_all(
        local_out.reshape(seq_count, tok_dev, heads_local, HD).astype(jnp.bfloat16),
        "seq",
        0,
        0,
        tiled=True,
    ).astype(jnp.float32)
    part_max = stats[..., 0]
    row_max = jnp.max(part_max, 0)
    factors = jnp.exp(part_max - row_max[None])
    row_sum = jnp.sum(stats[..., 1] * factors, 0)
    weighted = jnp.sum(parts_out * factors[..., None], 0)
    attended = (
        (weighted / row_sum[..., None]).astype(jnp.bfloat16).reshape(tok_dev, heads_local * HD)
    )
    projected = jnp.dot(attended, out_proj, preferred_element_type=jnp.float32)
    attn_out = lax.psum_scatter(
        projected.astype(jnp.bfloat16), "tensor", scatter_dimension=1, tiled=True
    ).astype(jnp.float32)
    stream = residual.astype(jnp.float32) + attn_out
    square_total = lax.psum(jnp.sum(stream * stream, 1), "tensor")
    inverse_rms = lax.rsqrt(square_total / D + epsilon)
    normed = (stream * inverse_rms[:, None] * norm_gain).astype(jnp.bfloat16)
    logits = lax.psum(
        jnp.dot(normed, router, preferred_element_type=jnp.float32).astype(jnp.bfloat16), "tensor"
    ).astype(jnp.float32)
    matches = expert_ids[:, :, None] == lax.iota(jnp.int32, experts)[None, None, :]
    selected = jnp.sum(jnp.where(matches, logits[:, None, :], 0.0), 2)
    sigmoids = jax.nn.sigmoid(selected)
    gates = sigmoids / jnp.sum(sigmoids, 1, keepdims=True)
    normed_full = lax.all_gather(normed, "tensor", axis=1, tiled=True)
    shared_pair = jnp.einsum(
        "td,dcf->tcf", normed_full, shared_gate_up, preferred_element_type=jnp.float32
    )
    shared_act = (jax.nn.silu(shared_pair[:, 0]) * shared_pair[:, 1]).astype(jnp.bfloat16)
    shared_term = jnp.dot(shared_act, shared_down, preferred_element_type=jnp.float32)
    shared_out = lax.psum_scatter(
        shared_term.astype(jnp.bfloat16), "tensor", scatter_dimension=1, tiled=True
    ).astype(jnp.float32)
    cap = tensor_count * (
        (4 * tok_dev * topk + 3 * experts * tensor_count - 1) // (3 * experts * tensor_count)
    )
    flat_ids = expert_ids.reshape(-1)
    marks = (flat_ids[:, None] == lax.iota(jnp.int32, experts)[None, :]).astype(jnp.int32)
    earlier = jnp.cumsum(marks, 0) - marks
    rank = jnp.sum(earlier * marks, 1)
    slot_index = flat_ids * cap + rank
    source_rows = (
        jnp.full((experts * cap,), tok_dev, jnp.int32)
        .at[slot_index]
        .set(lax.iota(jnp.int32, flat_ids.shape[0]) // topk)
    )
    padded_local = jnp.concatenate([normed, jnp.zeros((1, width_local), jnp.bfloat16)], 0)
    outgoing = padded_local[source_rows].reshape(seq_count, exp_dev, cap, width_local)
    incoming = lax.all_to_all(outgoing, "seq", split_axis=0, concat_axis=0, tiled=True)
    routed_rows = lax.all_gather(incoming, "tensor", axis=3, tiled=True)
    expert_pair = jnp.einsum(
        "secd,edjf->secjf", routed_rows, expert_gate_up, preferred_element_type=jnp.float32
    )
    expert_act = (jax.nn.silu(expert_pair[..., 0, :]) * expert_pair[..., 1, :]).astype(jnp.bfloat16)
    expert_term = jnp.einsum(
        "secf,efd->secd", expert_act, expert_down, preferred_element_type=jnp.float32
    )
    expert_total = lax.psum_scatter(
        expert_term.astype(jnp.bfloat16), "tensor", scatter_dimension=3, tiled=True
    )
    returned = lax.all_to_all(expert_total, "seq", split_axis=0, concat_axis=0, tiled=True)
    picked = returned.reshape(experts * cap, width_local)[slot_index].reshape(
        tok_dev, topk, width_local
    )
    mixture = jnp.sum(gates[..., None] * picked.astype(jnp.float32), 1)
    return (stream + shared_out + mixture).astype(jnp.bfloat16)


def solution(mesh):
    in_specs = (
        P("seq", "tensor"),
        P("seq", "tensor"),
        P("seq", "tensor"),
        P("seq", "tensor"),
        P(None, "seq", "tensor"),
        P(None, "seq", "tensor"),
        P(),
        P("tensor", None),
        P("tensor"),
        P("tensor", None),
        P("seq", None),
        P("seq", None, None, "tensor"),
        P("seq", "tensor", None),
        P(None, None, "tensor"),
        P("tensor", None),
    )
    out_specs = P("seq", "tensor")
    return jax.shard_map(shards, mesh=mesh, in_specs=in_specs, out_specs=out_specs, check_vma=False)
```

```python
import math

import jax
import jax.numpy as jnp
from jax import lax
from jax.sharding import PartitionSpec as P

D = 2048
HD = 128
NEW = 512


negative = -1e30
epsilon = 1e-06


def block_partial(scores, visible, values):
    masked = jnp.where(visible, scores, negative)
    block_max = jnp.max(masked, -1)
    shifted = jnp.where(visible, scores, block_max[..., None]) - block_max[..., None]
    weights = jnp.where(visible, jnp.exp(shifted), 0.0)
    block_sum = jnp.sum(weights, -1)
    block_out = jnp.einsum(
        "hqk,khd->qhd", weights.astype(jnp.bfloat16), values, preferred_element_type=jnp.float32
    )
    return (block_max, block_sum, block_out)


def shards(
    residual,
    queries,
    new_keys,
    new_values,
    cache_keys,
    cache_values,
    cache_lengths,
    out_proj,
    norm_gain,
    router,
    expert_ids,
    expert_gate_up,
    expert_down,
    shared_gate_up,
    shared_down,
):
    seq_count = lax.axis_size("seq")
    tensor_count = lax.axis_size("tensor")
    seq_index = lax.axis_index("seq")
    tok_dev = queries.shape[0]
    heads_local = queries.shape[1] // HD
    requests = tok_dev * seq_count // NEW
    clen_dev = cache_keys.shape[1]
    tokens = tok_dev * seq_count
    width_local = residual.shape[1]
    experts = router.shape[1]
    exp_dev = expert_gate_up.shape[0]
    topk = expert_ids.shape[1]
    scaling = 1.0 / math.sqrt(HD)
    spread = jnp.broadcast_to(queries[None], (seq_count,) + queries.shape)
    every_query = lax.all_to_all(spread, "seq", 0, 0, tiled=True).reshape(tokens, width_local)
    grouped = every_query.reshape(requests, NEW, heads_local, HD)
    first_place = seq_index * clen_dev

    cached_scores = (
        jnp.einsum(
            "rqhd,rkhd->rhqk",
            grouped,
            cache_keys.reshape(requests, clen_dev, heads_local, HD),
            preferred_element_type=jnp.float32,
        )
        * scaling
    )
    cached_visible = (
        first_place + lax.iota(jnp.int32, clen_dev)[None, :] < cache_lengths[:, None]
    )[:, None, None, :]
    masked = jnp.where(cached_visible, cached_scores, negative)
    max_cached = jnp.max(masked, -1)
    cached_weights = jnp.where(
        cached_visible, jnp.exp(cached_scores - max_cached[..., None]), 0.0
    )
    sum_cached = jnp.sum(cached_weights, -1)
    out_cached = jnp.einsum(
        "rhqk,rkhd->rqhd",
        cached_weights.astype(jnp.bfloat16),
        cache_values.reshape(requests, clen_dev, heads_local, HD),
        preferred_element_type=jnp.float32,
    )
    max_cached = jnp.transpose(max_cached, (0, 2, 1))
    sum_cached = jnp.transpose(sum_cached, (0, 2, 1))
    own_start = seq_index * tok_dev
    own_request = own_start // NEW
    offset = own_start % NEW
    own_queries = lax.dynamic_index_in_dim(grouped, own_request, 0, keepdims=False)
    new_scores = (
        jnp.einsum(
            "qhd,khd->hqk",
            own_queries,
            new_keys.reshape(tok_dev, heads_local, HD),
            preferred_element_type=jnp.float32,
        )
        * scaling
    )
    visible_new = (
        lax.iota(jnp.int32, NEW)[:, None] >= offset + lax.iota(jnp.int32, tok_dev)[None, :]
    )[None]
    max_new, sum_new, out_new = block_partial(
        new_scores, visible_new, new_values.reshape(tok_dev, heads_local, HD)
    )
    chosen_request = (lax.iota(jnp.int32, requests) == own_request)[:, None, None]
    max_placed = jnp.where(chosen_request, jnp.transpose(max_new)[None], negative)
    sum_placed = jnp.where(chosen_request, jnp.transpose(sum_new)[None], 0.0)
    out_placed = jnp.where(chosen_request[..., None], out_new[None], 0.0)
    local_max = jnp.maximum(max_cached, max_placed)
    factor_cached = jnp.exp(max_cached - local_max)
    factor_new = jnp.exp(max_placed - local_max)
    local_sum = sum_cached * factor_cached + sum_placed * factor_new
    local_out = out_cached * factor_cached[..., None] + out_placed * factor_new[..., None]
    flat_max = local_max.reshape(seq_count, tok_dev, heads_local)
    flat_sum = local_sum.reshape(seq_count, tok_dev, heads_local)
    stats = lax.all_to_all(
        jnp.stack([flat_max, flat_sum], -1), "seq", 0, 0, tiled=True
    )
    parts_out = lax.all_to_all(
        local_out.reshape(seq_count, tok_dev, heads_local, HD).astype(jnp.bfloat16),
        "seq",
        0,
        0,
        tiled=True,
    ).astype(jnp.float32)
    part_max = stats[..., 0]
    row_max = jnp.max(part_max, 0)
    factors = jnp.exp(part_max - row_max[None])
    row_sum = jnp.sum(stats[..., 1] * factors, 0)
    weighted = jnp.sum(parts_out * factors[..., None], 0)
    attended = (
        (weighted / row_sum[..., None]).astype(jnp.bfloat16).reshape(tok_dev, heads_local * HD)
    )
    projected = jnp.dot(attended, out_proj, preferred_element_type=jnp.float32)
    attn_out = lax.psum_scatter(
        projected.astype(jnp.bfloat16), "tensor", scatter_dimension=1, tiled=True
    ).astype(jnp.float32)
    stream = residual.astype(jnp.float32) + attn_out
    square_total = lax.psum(jnp.sum(stream * stream, 1), "tensor")
    inverse_rms = lax.rsqrt(square_total / D + epsilon)
    normed = (stream * inverse_rms[:, None] * norm_gain).astype(jnp.bfloat16)
    logits = lax.psum(
        jnp.dot(normed, router, preferred_element_type=jnp.float32).astype(jnp.bfloat16), "tensor"
    ).astype(jnp.float32)
    matches = expert_ids[:, :, None] == lax.iota(jnp.int32, experts)[None, None, :]
    selected = jnp.sum(jnp.where(matches, logits[:, None, :], 0.0), 2)
    sigmoids = jax.nn.sigmoid(selected)
    gates = sigmoids / jnp.sum(sigmoids, 1, keepdims=True)
    normed_full = lax.all_gather(normed, "tensor", axis=1, tiled=True)
    shared_pair = jnp.einsum(
        "td,dcf->tcf", normed_full, shared_gate_up, preferred_element_type=jnp.float32
    )
    shared_act = (jax.nn.silu(shared_pair[:, 0]) * shared_pair[:, 1]).astype(jnp.bfloat16)
    shared_term = jnp.dot(shared_act, shared_down, preferred_element_type=jnp.float32)
    shared_out = lax.psum_scatter(
        shared_term.astype(jnp.bfloat16), "tensor", scatter_dimension=1, tiled=True
    ).astype(jnp.float32)
    cap = tensor_count * (
        (4 * tok_dev * topk + 3 * experts * tensor_count - 1) // (3 * experts * tensor_count)
    )
    flat_ids = expert_ids.reshape(-1)
    marks = (flat_ids[:, None] == lax.iota(jnp.int32, experts)[None, :]).astype(jnp.int32)
    earlier = jnp.cumsum(marks, 0) - marks
    rank = jnp.sum(earlier * marks, 1)
    slot_index = flat_ids * cap + rank
    source_rows = (
        jnp.full((experts * cap,), tok_dev, jnp.int32)
        .at[slot_index]
        .set(lax.iota(jnp.int32, flat_ids.shape[0]) // topk)
    )
    padded_local = jnp.concatenate([normed, jnp.zeros((1, width_local), jnp.bfloat16)], 0)
    outgoing = padded_local[source_rows].reshape(seq_count, exp_dev, cap, width_local)
    incoming = lax.all_to_all(outgoing, "seq", split_axis=0, concat_axis=0, tiled=True)
    routed_rows = lax.all_gather(incoming, "tensor", axis=3, tiled=True)
    expert_pair = jnp.einsum(
        "secd,edjf->secjf", routed_rows, expert_gate_up, preferred_element_type=jnp.float32
    )
    expert_act = (jax.nn.silu(expert_pair[..., 0, :]) * expert_pair[..., 1, :]).astype(jnp.bfloat16)
    expert_term = jnp.einsum(
        "secf,efd->secd", expert_act, expert_down, preferred_element_type=jnp.float32
    )
    expert_total = lax.psum_scatter(
        expert_term.astype(jnp.bfloat16), "tensor", scatter_dimension=3, tiled=True
    )
    returned = lax.all_to_all(expert_total, "seq", split_axis=0, concat_axis=0, tiled=True)
    picked = returned.reshape(experts * cap, width_local)[slot_index].reshape(
        tok_dev, topk, width_local
    )
    mixture = jnp.sum(gates[..., None] * picked.astype(jnp.float32), 1)
    return (stream + shared_out + mixture).astype(jnp.bfloat16)


def solution(mesh):
    in_specs = (
        P("seq", "tensor"),
        P("seq", "tensor"),
        P("seq", "tensor"),
        P("seq", "tensor"),
        P(None, "seq", "tensor"),
        P(None, "seq", "tensor"),
        P(),
        P("tensor", None),
        P("tensor"),
        P("tensor", None),
        P("seq", None),
        P("seq", None, None, "tensor"),
        P("seq", "tensor", None),
        P(None, None, "tensor"),
        P("tensor", None),
    )
    out_specs = P("seq", "tensor")
    return jax.shard_map(shards, mesh=mesh, in_specs=in_specs, out_specs=out_specs, check_vma=False)
```

```python
import math

import jax
import jax.numpy as jnp
from jax import lax
from jax.sharding import PartitionSpec as P

D = 2048
HD = 128
NEW = 512


negative = -1e30
epsilon = 1e-06


def block_partial(scores, visible, values):
    masked = jnp.where(visible, scores, negative)
    block_max = jnp.max(masked, -1)
    shifted = jnp.where(visible, scores, block_max[..., None]) - block_max[..., None]
    weights = jnp.where(visible, jnp.exp(shifted), 0.0)
    block_sum = jnp.sum(weights, -1)
    block_out = jnp.einsum(
        "hqk,khd->qhd", weights.astype(jnp.bfloat16), values, preferred_element_type=jnp.float32
    )
    return (block_max, block_sum, block_out)


def shards(
    residual,
    queries,
    new_keys,
    new_values,
    cache_keys,
    cache_values,
    cache_lengths,
    out_proj,
    norm_gain,
    router,
    expert_ids,
    expert_gate_up,
    expert_down,
    shared_gate_up,
    shared_down,
):
    seq_count = lax.axis_size("seq")
    tensor_count = lax.axis_size("tensor")
    seq_index = lax.axis_index("seq")
    tok_dev = queries.shape[0]
    heads_local = queries.shape[1] // HD
    requests = tok_dev * seq_count // NEW
    clen_dev = cache_keys.shape[1]
    tokens = tok_dev * seq_count
    width_local = residual.shape[1]
    experts = router.shape[1]
    exp_dev = expert_gate_up.shape[0]
    topk = expert_ids.shape[1]
    scaling = 1.0 / math.sqrt(HD)
    spread = jnp.broadcast_to(queries[None], (seq_count,) + queries.shape)
    every_query = lax.all_to_all(spread, "seq", 0, 0, tiled=True).reshape(tokens, width_local)
    grouped = every_query.reshape(requests, NEW, heads_local, HD)
    first_place = seq_index * clen_dev

    cached_scores = (
        jnp.einsum(
            "rqhd,rkhd->rhqk",
            grouped,
            cache_keys.reshape(requests, clen_dev, heads_local, HD),
            preferred_element_type=jnp.float32,
        )
        * scaling
    )
    cached_visible = (
        first_place + lax.iota(jnp.int32, clen_dev)[None, :] < cache_lengths[:, None]
    )[:, None, None, :]
    masked = jnp.where(cached_visible, cached_scores, negative)
    max_cached = jnp.max(masked, -1)
    cached_weights = jnp.where(
        cached_visible, jnp.exp(cached_scores - max_cached[..., None]), 0.0
    )
    sum_cached = jnp.sum(cached_weights, -1)
    out_cached = jnp.einsum(
        "rhqk,rkhd->rqhd",
        cached_weights.astype(jnp.bfloat16),
        cache_values.reshape(requests, clen_dev, heads_local, HD),
        preferred_element_type=jnp.float32,
    )
    max_cached = jnp.transpose(max_cached, (0, 2, 1))
    sum_cached = jnp.transpose(sum_cached, (0, 2, 1))
    own_start = seq_index * tok_dev
    own_request = own_start // NEW
    offset = own_start % NEW
    own_queries = lax.dynamic_index_in_dim(grouped, own_request, 0, keepdims=False)
    new_scores = (
        jnp.einsum(
            "qhd,khd->hqk",
            own_queries,
            new_keys.reshape(tok_dev, heads_local, HD),
            preferred_element_type=jnp.float32,
        )
        * scaling
    )
    visible_new = (
        lax.iota(jnp.int32, NEW)[:, None] >= offset + lax.iota(jnp.int32, tok_dev)[None, :]
    )[None]
    max_new, sum_new, out_new = block_partial(
        new_scores, visible_new, new_values.reshape(tok_dev, heads_local, HD)
    )
    chosen_request = (lax.iota(jnp.int32, requests) == own_request)[:, None, None]
    max_placed = jnp.where(chosen_request, jnp.transpose(max_new)[None], negative)
    sum_placed = jnp.where(chosen_request, jnp.transpose(sum_new)[None], 0.0)
    out_placed = jnp.where(chosen_request[..., None], out_new[None], 0.0)
    local_max = jnp.maximum(max_cached, max_placed)
    factor_cached = jnp.exp(max_cached - local_max)
    factor_new = jnp.exp(max_placed - local_max)
    local_sum = sum_cached * factor_cached + sum_placed * factor_new
    local_out = out_cached * factor_cached[..., None] + out_placed * factor_new[..., None]
    flat_max = local_max.reshape(seq_count, tok_dev, heads_local)
    flat_sum = local_sum.reshape(seq_count, tok_dev, heads_local)
    stats = lax.all_to_all(
        jnp.stack([flat_max, flat_sum], -1), "seq", 0, 0, tiled=True
    )
    parts_out = lax.all_to_all(
        local_out.reshape(seq_count, tok_dev, heads_local, HD).astype(jnp.bfloat16),
        "seq",
        0,
        0,
        tiled=True,
    ).astype(jnp.float32)
    part_max = stats[..., 0]
    row_max = jnp.max(part_max, 0)
    factors = jnp.exp(part_max - row_max[None])
    row_sum = jnp.sum(stats[..., 1] * factors, 0)
    weighted = jnp.sum(parts_out * factors[..., None], 0)
    attended = (
        (weighted / row_sum[..., None]).astype(jnp.bfloat16).reshape(tok_dev, heads_local * HD)
    )
    tensor_index = lax.axis_index("tensor")
    own_slice = (lax.iota(jnp.int32, tensor_count) == tensor_index)[None, :, None]

    def placed(part):
        return jnp.where(own_slice, part[:, None, :], 0.0).reshape(part.shape[0], -1)

    weights_full = lax.psum(
        placed(jnp.concatenate([router.astype(jnp.float32).T, norm_gain[None]], 0)), "tensor"
    )
    router_full = weights_full[:experts].T.astype(jnp.bfloat16)
    gain_full = weights_full[experts]
    projected = jnp.dot(attended, out_proj, preferred_element_type=jnp.float32)
    stream_full = lax.psum(projected + placed(residual.astype(jnp.float32)), "tensor")
    inverse_rms = lax.rsqrt(jnp.sum(stream_full * stream_full, 1) / D + epsilon)
    normed_full = (stream_full * inverse_rms[:, None] * gain_full).astype(jnp.bfloat16)
    stream = lax.dynamic_slice_in_dim(stream_full, tensor_index * width_local, width_local, 1)
    normed = lax.dynamic_slice_in_dim(normed_full, tensor_index * width_local, width_local, 1)
    logits = jnp.dot(normed_full, router_full, preferred_element_type=jnp.float32)
    matches = expert_ids[:, :, None] == lax.iota(jnp.int32, experts)[None, None, :]
    selected = jnp.sum(jnp.where(matches, logits[:, None, :], 0.0), 2)
    sigmoids = jax.nn.sigmoid(selected)
    gates = sigmoids / jnp.sum(sigmoids, 1, keepdims=True)
    shared_pair = jnp.einsum(
        "td,dcf->tcf", normed_full, shared_gate_up, preferred_element_type=jnp.float32
    )
    shared_act = (jax.nn.silu(shared_pair[:, 0]) * shared_pair[:, 1]).astype(jnp.bfloat16)
    shared_term = jnp.dot(shared_act, shared_down, preferred_element_type=jnp.float32)
    shared_out = lax.psum_scatter(
        shared_term.astype(jnp.bfloat16), "tensor", scatter_dimension=1, tiled=True
    ).astype(jnp.float32)
    cap = tensor_count * (
        (4 * tok_dev * topk + 3 * experts * tensor_count - 1) // (3 * experts * tensor_count)
    )
    flat_ids = expert_ids.reshape(-1)
    marks = (flat_ids[:, None] == lax.iota(jnp.int32, experts)[None, :]).astype(jnp.int32)
    earlier = jnp.cumsum(marks, 0) - marks
    rank = jnp.sum(earlier * marks, 1)
    slot_index = flat_ids * cap + rank
    source_rows = (
        jnp.full((experts * cap,), tok_dev, jnp.int32)
        .at[slot_index]
        .set(lax.iota(jnp.int32, flat_ids.shape[0]) // topk)
    )
    padded_local = jnp.concatenate([normed, jnp.zeros((1, width_local), jnp.bfloat16)], 0)
    outgoing = padded_local[source_rows].reshape(seq_count, exp_dev, cap, width_local)
    incoming = lax.all_to_all(outgoing, "seq", split_axis=0, concat_axis=0, tiled=True)
    routed_rows = lax.all_gather(incoming, "tensor", axis=3, tiled=True)
    expert_pair = jnp.einsum(
        "secd,edjf->secjf", routed_rows, expert_gate_up, preferred_element_type=jnp.float32
    )
    expert_act = (jax.nn.silu(expert_pair[..., 0, :]) * expert_pair[..., 1, :]).astype(jnp.bfloat16)
    expert_term = jnp.einsum(
        "secf,efd->secd", expert_act, expert_down, preferred_element_type=jnp.float32
    )
    expert_total = lax.psum_scatter(
        expert_term.astype(jnp.bfloat16), "tensor", scatter_dimension=3, tiled=True
    )
    returned = lax.all_to_all(expert_total, "seq", split_axis=0, concat_axis=0, tiled=True)
    picked = returned.reshape(experts * cap, width_local)[slot_index].reshape(
        tok_dev, topk, width_local
    )
    mixture = jnp.sum(gates[..., None] * picked.astype(jnp.float32), 1)
    return (stream + shared_out + mixture).astype(jnp.bfloat16)


def solution(mesh):
    in_specs = (
        P("seq", "tensor"),
        P("seq", "tensor"),
        P("seq", "tensor"),
        P("seq", "tensor"),
        P(None, "seq", "tensor"),
        P(None, "seq", "tensor"),
        P(),
        P("tensor", None),
        P("tensor"),
        P("tensor", None),
        P("seq", None),
        P("seq", None, None, "tensor"),
        P("seq", "tensor", None),
        P(None, None, "tensor"),
        P("tensor", None),
    )
    out_specs = P("seq", "tensor")
    return jax.shard_map(shards, mesh=mesh, in_specs=in_specs, out_specs=out_specs, check_vma=False)
```

```python
import math

import jax
import jax.numpy as jnp
from jax import lax
from jax.sharding import PartitionSpec as P

D = 2048
HD = 128
NEW = 512


negative = -1e30
epsilon = 1e-06


def block_partial(scores, visible, values):
    masked = jnp.where(visible, scores, negative)
    block_max = jnp.max(masked, -1)
    shifted = jnp.where(visible, scores, block_max[..., None]) - block_max[..., None]
    weights = jnp.where(visible, jnp.exp(shifted), 0.0)
    block_sum = jnp.sum(weights, -1)
    block_out = jnp.einsum(
        "hqk,khd->qhd", weights.astype(jnp.bfloat16), values, preferred_element_type=jnp.float32
    )
    return (block_max, block_sum, block_out)


def shards(
    residual,
    queries,
    new_keys,
    new_values,
    cache_keys,
    cache_values,
    cache_lengths,
    out_proj,
    norm_gain,
    router,
    expert_ids,
    expert_gate_up,
    expert_down,
    shared_gate_up,
    shared_down,
):
    seq_count = lax.axis_size("seq")
    tensor_count = lax.axis_size("tensor")
    seq_index = lax.axis_index("seq")
    tok_dev = queries.shape[0]
    heads_local = queries.shape[1] // HD
    requests = tok_dev * seq_count // NEW
    clen_dev = cache_keys.shape[1]
    tokens = tok_dev * seq_count
    width_local = residual.shape[1]
    experts = router.shape[1]
    exp_dev = expert_gate_up.shape[0]
    topk = expert_ids.shape[1]
    scaling = 1.0 / math.sqrt(HD)
    spread = jnp.broadcast_to(queries[None], (seq_count,) + queries.shape)
    every_query = lax.all_to_all(spread, "seq", 0, 0, tiled=True).reshape(tokens, width_local)
    grouped = every_query.reshape(requests, NEW, heads_local, HD)
    first_place = seq_index * clen_dev

    cached_scores = (
        jnp.einsum(
            "rqhd,rkhd->rhqk",
            grouped,
            cache_keys.reshape(requests, clen_dev, heads_local, HD),
            preferred_element_type=jnp.float32,
        )
        * scaling
    )
    cached_visible = (
        first_place + lax.iota(jnp.int32, clen_dev)[None, :] < cache_lengths[:, None]
    )[:, None, None, :]
    masked = jnp.where(cached_visible, cached_scores, negative)
    max_cached = jnp.max(masked, -1)
    cached_weights = jnp.where(
        cached_visible, jnp.exp(cached_scores - max_cached[..., None]), 0.0
    )
    sum_cached = jnp.sum(cached_weights, -1)
    out_cached = jnp.einsum(
        "rhqk,rkhd->rqhd",
        cached_weights.astype(jnp.bfloat16),
        cache_values.reshape(requests, clen_dev, heads_local, HD),
        preferred_element_type=jnp.float32,
    )
    max_cached = jnp.transpose(max_cached, (0, 2, 1))
    sum_cached = jnp.transpose(sum_cached, (0, 2, 1))
    own_start = seq_index * tok_dev
    own_request = own_start // NEW
    offset = own_start % NEW
    own_queries = lax.dynamic_index_in_dim(grouped, own_request, 0, keepdims=False)
    new_scores = (
        jnp.einsum(
            "qhd,khd->hqk",
            own_queries,
            new_keys.reshape(tok_dev, heads_local, HD),
            preferred_element_type=jnp.float32,
        )
        * scaling
    )
    visible_new = (
        lax.iota(jnp.int32, NEW)[:, None] >= offset + lax.iota(jnp.int32, tok_dev)[None, :]
    )[None]
    max_new, sum_new, out_new = block_partial(
        new_scores, visible_new, new_values.reshape(tok_dev, heads_local, HD)
    )
    chosen_request = (lax.iota(jnp.int32, requests) == own_request)[:, None, None]
    max_placed = jnp.where(chosen_request, jnp.transpose(max_new)[None], negative)
    sum_placed = jnp.where(chosen_request, jnp.transpose(sum_new)[None], 0.0)
    out_placed = jnp.where(chosen_request[..., None], out_new[None], 0.0)
    local_max = jnp.maximum(max_cached, max_placed)
    factor_cached = jnp.exp(max_cached - local_max)
    factor_new = jnp.exp(max_placed - local_max)
    local_sum = sum_cached * factor_cached + sum_placed * factor_new
    local_out = out_cached * factor_cached[..., None] + out_placed * factor_new[..., None]
    flat_max = local_max.reshape(seq_count, tok_dev, heads_local)
    flat_sum = local_sum.reshape(seq_count, tok_dev, heads_local)
    stats = lax.all_to_all(
        jnp.stack([flat_max, flat_sum], -1), "seq", 0, 0, tiled=True
    )
    parts_out = lax.all_to_all(
        local_out.reshape(seq_count, tok_dev, heads_local, HD).astype(jnp.bfloat16),
        "seq",
        0,
        0,
        tiled=True,
    ).astype(jnp.float32)
    part_max = stats[..., 0]
    row_max = jnp.max(part_max, 0)
    factors = jnp.exp(part_max - row_max[None])
    row_sum = jnp.sum(stats[..., 1] * factors, 0)
    weighted = jnp.sum(parts_out * factors[..., None], 0)
    attended = (
        (weighted / row_sum[..., None]).astype(jnp.bfloat16).reshape(tok_dev, heads_local * HD)
    )
    projected = jnp.dot(attended, out_proj, preferred_element_type=jnp.float32)
    attn_out = lax.psum_scatter(
        projected.astype(jnp.bfloat16), "tensor", scatter_dimension=1, tiled=True
    ).astype(jnp.float32)
    stream = residual.astype(jnp.float32) + attn_out
    gathered = lax.all_gather(
        jnp.concatenate([stream, norm_gain[None], router.astype(jnp.float32).T], 0),
        "tensor",
        axis=1,
        tiled=True,
    )
    stream_full = gathered[:tok_dev]
    gain_full = gathered[tok_dev]
    router_full = gathered[tok_dev + 1 :].T.astype(jnp.bfloat16)
    inverse_rms = lax.rsqrt(jnp.sum(stream_full * stream_full, 1) / D + epsilon)
    normed_full = (stream_full * inverse_rms[:, None] * gain_full).astype(jnp.bfloat16)
    normed = (stream * inverse_rms[:, None] * norm_gain).astype(jnp.bfloat16)
    logits = jnp.dot(normed_full, router_full, preferred_element_type=jnp.float32)
    matches = expert_ids[:, :, None] == lax.iota(jnp.int32, experts)[None, None, :]
    selected = jnp.sum(jnp.where(matches, logits[:, None, :], 0.0), 2)
    sigmoids = jax.nn.sigmoid(selected)
    gates = sigmoids / jnp.sum(sigmoids, 1, keepdims=True)
    shared_pair = jnp.einsum(
        "td,dcf->tcf", normed_full, shared_gate_up, preferred_element_type=jnp.float32
    )
    shared_act = (jax.nn.silu(shared_pair[:, 0]) * shared_pair[:, 1]).astype(jnp.bfloat16)
    shared_term = jnp.dot(shared_act, shared_down, preferred_element_type=jnp.float32)
    shared_out = lax.psum_scatter(
        shared_term.astype(jnp.bfloat16), "tensor", scatter_dimension=1, tiled=True
    ).astype(jnp.float32)
    cap = tensor_count * (
        (4 * tok_dev * topk + 3 * experts * tensor_count - 1) // (3 * experts * tensor_count)
    )
    flat_ids = expert_ids.reshape(-1)
    marks = (flat_ids[:, None] == lax.iota(jnp.int32, experts)[None, :]).astype(jnp.int32)
    earlier = jnp.cumsum(marks, 0) - marks
    rank = jnp.sum(earlier * marks, 1)
    slot_index = flat_ids * cap + rank
    source_rows = (
        jnp.full((experts * cap,), tok_dev, jnp.int32)
        .at[slot_index]
        .set(lax.iota(jnp.int32, flat_ids.shape[0]) // topk)
    )
    padded_local = jnp.concatenate([normed, jnp.zeros((1, width_local), jnp.bfloat16)], 0)
    outgoing = padded_local[source_rows].reshape(seq_count, exp_dev, cap, width_local)
    incoming = lax.all_to_all(outgoing, "seq", split_axis=0, concat_axis=0, tiled=True)
    routed_rows = lax.all_gather(incoming, "tensor", axis=3, tiled=True)
    expert_pair = jnp.einsum(
        "secd,edjf->secjf", routed_rows, expert_gate_up, preferred_element_type=jnp.float32
    )
    expert_act = (jax.nn.silu(expert_pair[..., 0, :]) * expert_pair[..., 1, :]).astype(jnp.bfloat16)
    expert_term = jnp.einsum(
        "secf,efd->secd", expert_act, expert_down, preferred_element_type=jnp.float32
    )
    expert_total = lax.psum_scatter(
        expert_term.astype(jnp.bfloat16), "tensor", scatter_dimension=3, tiled=True
    )
    returned = lax.all_to_all(expert_total, "seq", split_axis=0, concat_axis=0, tiled=True)
    picked = returned.reshape(experts * cap, width_local)[slot_index].reshape(
        tok_dev, topk, width_local
    )
    mixture = jnp.sum(gates[..., None] * picked.astype(jnp.float32), 1)
    return (stream + shared_out + mixture).astype(jnp.bfloat16)


def solution(mesh):
    in_specs = (
        P("seq", "tensor"),
        P("seq", "tensor"),
        P("seq", "tensor"),
        P("seq", "tensor"),
        P(None, "seq", "tensor"),
        P(None, "seq", "tensor"),
        P(),
        P("tensor", None),
        P("tensor"),
        P("tensor", None),
        P("seq", None),
        P("seq", None, None, "tensor"),
        P("seq", "tensor", None),
        P(None, None, "tensor"),
        P("tensor", None),
    )
    out_specs = P("seq", "tensor")
    return jax.shard_map(shards, mesh=mesh, in_specs=in_specs, out_specs=out_specs, check_vma=False)
```

```python
import math

import jax
import jax.numpy as jnp
from jax import lax
from jax.sharding import PartitionSpec as P

D = 2048
HD = 128
NEW = 512


negative = -1e30
epsilon = 1e-06


def block_partial(scores, visible, values):
    masked = jnp.where(visible, scores, negative)
    block_max = jnp.max(masked, -1)
    shifted = jnp.where(visible, scores, block_max[..., None]) - block_max[..., None]
    weights = jnp.where(visible, jnp.exp(shifted), 0.0)
    block_sum = jnp.sum(weights, -1)
    block_out = jnp.einsum(
        "hqk,khd->qhd", weights.astype(jnp.bfloat16), values, preferred_element_type=jnp.float32
    )
    return (block_max, block_sum, block_out)


def shards(
    residual,
    queries,
    new_keys,
    new_values,
    cache_keys,
    cache_values,
    cache_lengths,
    out_proj,
    norm_gain,
    router,
    expert_ids,
    expert_gate_up,
    expert_down,
    shared_gate_up,
    shared_down,
):
    seq_count = lax.axis_size("seq")
    tensor_count = lax.axis_size("tensor")
    seq_index = lax.axis_index("seq")
    tok_dev = queries.shape[0]
    heads_local = queries.shape[1] // HD
    requests = tok_dev * seq_count // NEW
    clen_dev = cache_keys.shape[1]
    tokens = tok_dev * seq_count
    width_local = residual.shape[1]
    experts = router.shape[1]
    exp_dev = expert_gate_up.shape[0]
    topk = expert_ids.shape[1]
    scaling = 1.0 / math.sqrt(HD)
    spread = jnp.broadcast_to(queries[None], (seq_count,) + queries.shape)
    every_query = lax.all_to_all(spread, "seq", 0, 0, tiled=True).reshape(tokens, width_local)
    grouped = every_query.reshape(requests, NEW, heads_local, HD)
    first_place = seq_index * clen_dev

    cached_scores = (
        jnp.einsum(
            "rqhd,rkhd->rhqk",
            grouped,
            cache_keys.reshape(requests, clen_dev, heads_local, HD),
            preferred_element_type=jnp.float32,
        )
        * scaling
    )
    cached_visible = (
        first_place + lax.iota(jnp.int32, clen_dev)[None, :] < cache_lengths[:, None]
    )[:, None, None, :]
    masked = jnp.where(cached_visible, cached_scores, negative)
    max_cached = jnp.max(masked, -1)
    cached_weights = jnp.where(
        cached_visible, jnp.exp(cached_scores - max_cached[..., None]), 0.0
    )
    sum_cached = jnp.sum(cached_weights, -1)
    out_cached = jnp.einsum(
        "rhqk,rkhd->rqhd",
        cached_weights.astype(jnp.bfloat16),
        cache_values.reshape(requests, clen_dev, heads_local, HD),
        preferred_element_type=jnp.float32,
    )
    max_cached = jnp.transpose(max_cached, (0, 2, 1))
    sum_cached = jnp.transpose(sum_cached, (0, 2, 1))
    own_start = seq_index * tok_dev
    own_request = own_start // NEW
    offset = own_start % NEW
    own_queries = lax.dynamic_index_in_dim(grouped, own_request, 0, keepdims=False)
    new_scores = (
        jnp.einsum(
            "qhd,khd->hqk",
            own_queries,
            new_keys.reshape(tok_dev, heads_local, HD),
            preferred_element_type=jnp.float32,
        )
        * scaling
    )
    visible_new = (
        lax.iota(jnp.int32, NEW)[:, None] >= offset + lax.iota(jnp.int32, tok_dev)[None, :]
    )[None]
    max_new, sum_new, out_new = block_partial(
        new_scores, visible_new, new_values.reshape(tok_dev, heads_local, HD)
    )
    chosen_request = (lax.iota(jnp.int32, requests) == own_request)[:, None, None]
    max_placed = jnp.where(chosen_request, jnp.transpose(max_new)[None], negative)
    sum_placed = jnp.where(chosen_request, jnp.transpose(sum_new)[None], 0.0)
    out_placed = jnp.where(chosen_request[..., None], out_new[None], 0.0)
    local_max = jnp.maximum(max_cached, max_placed)
    factor_cached = jnp.exp(max_cached - local_max)
    factor_new = jnp.exp(max_placed - local_max)
    local_sum = sum_cached * factor_cached + sum_placed * factor_new
    local_out = out_cached * factor_cached[..., None] + out_placed * factor_new[..., None]
    flat_max = local_max.reshape(seq_count, tok_dev, heads_local)
    flat_sum = local_sum.reshape(seq_count, tok_dev, heads_local)
    stats = lax.all_to_all(
        jnp.stack([flat_max, flat_sum], -1), "seq", 0, 0, tiled=True
    )
    parts_out = lax.all_to_all(
        local_out.reshape(seq_count, tok_dev, heads_local, HD).astype(jnp.bfloat16),
        "seq",
        0,
        0,
        tiled=True,
    ).astype(jnp.float32)
    part_max = stats[..., 0]
    row_max = jnp.max(part_max, 0)
    factors = jnp.exp(part_max - row_max[None])
    row_sum = jnp.sum(stats[..., 1] * factors, 0)
    weighted = jnp.sum(parts_out * factors[..., None], 0)
    attended = (
        (weighted / row_sum[..., None]).astype(jnp.bfloat16).reshape(tok_dev, heads_local * HD)
    )
    projected = jnp.dot(attended, out_proj, preferred_element_type=jnp.float32)
    attn_out = lax.psum_scatter(
        projected.astype(jnp.bfloat16), "tensor", scatter_dimension=1, tiled=True
    ).astype(jnp.float32)
    stream = residual.astype(jnp.float32) + attn_out
    gathered = lax.all_gather(
        jnp.concatenate([stream, norm_gain[None], router.astype(jnp.float32).T], 0),
        "tensor",
        axis=1,
        tiled=True,
    )
    stream_full = gathered[:tok_dev]
    gain_full = gathered[tok_dev]
    router_full = gathered[tok_dev + 1 :].T.astype(jnp.bfloat16)
    inverse_rms = lax.rsqrt(jnp.sum(stream_full * stream_full, 1) / D + epsilon)
    normed_full = (stream_full * inverse_rms[:, None] * gain_full).astype(jnp.bfloat16)
    normed = (stream * inverse_rms[:, None] * norm_gain).astype(jnp.bfloat16)
    logits = jnp.dot(normed_full, router_full, preferred_element_type=jnp.float32)
    matches = expert_ids[:, :, None] == lax.iota(jnp.int32, experts)[None, None, :]
    selected = jnp.sum(jnp.where(matches, logits[:, None, :], 0.0), 2)
    sigmoids = jax.nn.sigmoid(selected)
    gates = sigmoids / jnp.sum(sigmoids, 1, keepdims=True)
    shared_pair = jnp.einsum(
        "td,dcf->tcf", normed_full, shared_gate_up, preferred_element_type=jnp.float32
    )
    shared_act = (jax.nn.silu(shared_pair[:, 0]) * shared_pair[:, 1]).astype(jnp.bfloat16)
    shared_term = jnp.dot(shared_act, shared_down, preferred_element_type=jnp.float32)
    shared_term, normed = lax.optimization_barrier((shared_term.astype(jnp.bfloat16), normed))
    shared_out = lax.psum_scatter(shared_term, "tensor", scatter_dimension=1, tiled=True)
    cap = tensor_count * (
        (4 * tok_dev * topk + 3 * experts * tensor_count - 1) // (3 * experts * tensor_count)
    )
    flat_ids = expert_ids.reshape(-1)
    marks = (flat_ids[:, None] == lax.iota(jnp.int32, experts)[None, :]).astype(jnp.int32)
    earlier = jnp.cumsum(marks, 0) - marks
    rank = jnp.sum(earlier * marks, 1)
    slot_index = flat_ids * cap + rank
    source_rows = (
        jnp.full((experts * cap,), tok_dev, jnp.int32)
        .at[slot_index]
        .set(lax.iota(jnp.int32, flat_ids.shape[0]) // topk)
    )
    padded_local = jnp.concatenate([normed, jnp.zeros((1, width_local), jnp.bfloat16)], 0)
    outgoing = padded_local[source_rows].reshape(seq_count, exp_dev, cap, width_local)
    incoming = lax.all_to_all(outgoing, "seq", split_axis=0, concat_axis=0, tiled=True)
    incoming, shared_out = lax.optimization_barrier((incoming, shared_out))
    routed_rows = lax.all_gather(incoming, "tensor", axis=3, tiled=True)
    expert_pair = jnp.einsum(
        "secd,edjf->secjf", routed_rows, expert_gate_up, preferred_element_type=jnp.float32
    )
    expert_act = (jax.nn.silu(expert_pair[..., 0, :]) * expert_pair[..., 1, :]).astype(jnp.bfloat16)
    expert_term = jnp.einsum(
        "secf,efd->secd", expert_act, expert_down, preferred_element_type=jnp.float32
    )
    expert_total = lax.psum_scatter(
        expert_term.astype(jnp.bfloat16), "tensor", scatter_dimension=3, tiled=True
    )
    returned = lax.all_to_all(expert_total, "seq", split_axis=0, concat_axis=0, tiled=True)
    picked = returned.reshape(experts * cap, width_local)[slot_index].reshape(
        tok_dev, topk, width_local
    )
    mixture = jnp.sum(gates[..., None] * picked.astype(jnp.float32), 1)
    return (stream + shared_out.astype(jnp.float32) + mixture).astype(jnp.bfloat16)


def solution(mesh):
    in_specs = (
        P("seq", "tensor"),
        P("seq", "tensor"),
        P("seq", "tensor"),
        P("seq", "tensor"),
        P(None, "seq", "tensor"),
        P(None, "seq", "tensor"),
        P(),
        P("tensor", None),
        P("tensor"),
        P("tensor", None),
        P("seq", None),
        P("seq", None, None, "tensor"),
        P("seq", "tensor", None),
        P(None, None, "tensor"),
        P("tensor", None),
    )
    out_specs = P("seq", "tensor")
    return jax.shard_map(shards, mesh=mesh, in_specs=in_specs, out_specs=out_specs, check_vma=False)
```

```python
import math

import jax
import jax.numpy as jnp
from jax import lax
from jax.sharding import PartitionSpec as P

D = 2048
HD = 128
NEW = 512


negative = -1e30
epsilon = 1e-06


def block_partial(scores, visible, values):
    masked = jnp.where(visible, scores, negative)
    block_max = jnp.max(masked, -1)
    shifted = jnp.where(visible, scores, block_max[..., None]) - block_max[..., None]
    weights = jnp.where(visible, jnp.exp(shifted), 0.0)
    block_sum = jnp.sum(weights, -1)
    block_out = jnp.einsum(
        "hqk,khd->qhd", weights.astype(jnp.bfloat16), values, preferred_element_type=jnp.float32
    )
    return (block_max, block_sum, block_out)


def shards(
    residual,
    queries,
    new_keys,
    new_values,
    cache_keys,
    cache_values,
    cache_lengths,
    out_proj,
    norm_gain,
    router,
    expert_ids,
    expert_gate_up,
    expert_down,
    shared_gate_up,
    shared_down,
):
    seq_count = lax.axis_size("seq")
    tensor_count = lax.axis_size("tensor")
    seq_index = lax.axis_index("seq")
    tok_dev = queries.shape[0]
    heads_local = queries.shape[1] // HD
    requests = tok_dev * seq_count // NEW
    clen_dev = cache_keys.shape[1]
    tokens = tok_dev * seq_count
    width_local = residual.shape[1]
    experts = router.shape[1]
    exp_dev = expert_gate_up.shape[0]
    topk = expert_ids.shape[1]
    scaling = 1.0 / math.sqrt(HD)
    spread = jnp.broadcast_to(queries[None], (seq_count,) + queries.shape)
    every_query = lax.all_to_all(spread, "seq", 0, 0, tiled=True).reshape(tokens, width_local)
    grouped = every_query.reshape(requests, NEW, heads_local, HD)
    first_place = seq_index * clen_dev

    cached_scores = (
        jnp.einsum(
            "rqhd,rkhd->rhqk",
            grouped,
            cache_keys.reshape(requests, clen_dev, heads_local, HD),
            preferred_element_type=jnp.float32,
        )
        * scaling
    )
    cached_visible = (
        first_place + lax.iota(jnp.int32, clen_dev)[None, :] < cache_lengths[:, None]
    )[:, None, None, :]
    masked = jnp.where(cached_visible, cached_scores, negative)
    max_cached = jnp.max(masked, -1)
    cached_weights = jnp.where(
        cached_visible, jnp.exp(cached_scores - max_cached[..., None]), 0.0
    )
    sum_cached = jnp.sum(cached_weights, -1)
    out_cached = jnp.einsum(
        "rhqk,rkhd->rqhd",
        cached_weights.astype(jnp.bfloat16),
        cache_values.reshape(requests, clen_dev, heads_local, HD),
        preferred_element_type=jnp.float32,
    )
    max_cached = jnp.transpose(max_cached, (0, 2, 1))
    sum_cached = jnp.transpose(sum_cached, (0, 2, 1))
    own_start = seq_index * tok_dev
    own_request = own_start // NEW
    offset = own_start % NEW
    own_queries = lax.dynamic_index_in_dim(grouped, own_request, 0, keepdims=False)
    new_scores = (
        jnp.einsum(
            "qhd,khd->hqk",
            own_queries,
            new_keys.reshape(tok_dev, heads_local, HD),
            preferred_element_type=jnp.float32,
        )
        * scaling
    )
    visible_new = (
        lax.iota(jnp.int32, NEW)[:, None] >= offset + lax.iota(jnp.int32, tok_dev)[None, :]
    )[None]
    max_new, sum_new, out_new = block_partial(
        new_scores, visible_new, new_values.reshape(tok_dev, heads_local, HD)
    )
    chosen_request = (lax.iota(jnp.int32, requests) == own_request)[:, None, None]
    max_placed = jnp.where(chosen_request, jnp.transpose(max_new)[None], negative)
    sum_placed = jnp.where(chosen_request, jnp.transpose(sum_new)[None], 0.0)
    out_placed = jnp.where(chosen_request[..., None], out_new[None], 0.0)
    local_max = jnp.maximum(max_cached, max_placed)
    factor_cached = jnp.exp(max_cached - local_max)
    factor_new = jnp.exp(max_placed - local_max)
    local_sum = sum_cached * factor_cached + sum_placed * factor_new
    local_out = out_cached * factor_cached[..., None] + out_placed * factor_new[..., None]
    flat_max = local_max.reshape(seq_count, tok_dev, heads_local)
    flat_sum = local_sum.reshape(seq_count, tok_dev, heads_local)
    stats = lax.all_to_all(
        jnp.stack([flat_max, flat_sum], -1), "seq", 0, 0, tiled=True
    )
    parts_out = lax.all_to_all(
        local_out.reshape(seq_count, tok_dev, heads_local, HD).astype(jnp.bfloat16),
        "seq",
        0,
        0,
        tiled=True,
    ).astype(jnp.float32)
    part_max = stats[..., 0]
    row_max = jnp.max(part_max, 0)
    factors = jnp.exp(part_max - row_max[None])
    row_sum = jnp.sum(stats[..., 1] * factors, 0)
    weighted = jnp.sum(parts_out * factors[..., None], 0)
    attended = (
        (weighted / row_sum[..., None]).astype(jnp.bfloat16).reshape(tok_dev, heads_local * HD)
    )
    projected = jnp.dot(attended, out_proj, preferred_element_type=jnp.float32)
    attn_out = lax.psum_scatter(
        projected.astype(jnp.bfloat16), "tensor", scatter_dimension=1, tiled=True
    ).astype(jnp.float32)
    stream = residual.astype(jnp.float32) + attn_out
    gathered = lax.all_gather(
        jnp.concatenate([stream, norm_gain[None], router.astype(jnp.float32).T], 0),
        "tensor",
        axis=1,
        tiled=True,
    )
    stream_full = gathered[:tok_dev]
    gain_full = gathered[tok_dev]
    router_full = gathered[tok_dev + 1 :].T.astype(jnp.bfloat16)
    inverse_rms = lax.rsqrt(jnp.sum(stream_full * stream_full, 1) / D + epsilon)
    normed_full = (stream_full * inverse_rms[:, None] * gain_full).astype(jnp.bfloat16)
    logits = jnp.dot(normed_full, router_full, preferred_element_type=jnp.float32)
    matches = expert_ids[:, :, None] == lax.iota(jnp.int32, experts)[None, None, :]
    selected = jnp.sum(jnp.where(matches, logits[:, None, :], 0.0), 2)
    sigmoids = jax.nn.sigmoid(selected)
    gates = sigmoids / jnp.sum(sigmoids, 1, keepdims=True)
    shared_pair = jnp.einsum(
        "td,dcf->tcf", normed_full, shared_gate_up, preferred_element_type=jnp.float32
    )
    shared_act = (jax.nn.silu(shared_pair[:, 0]) * shared_pair[:, 1]).astype(jnp.bfloat16)
    shared_term = jnp.dot(shared_act, shared_down, preferred_element_type=jnp.float32)
    shared_term, normed_full = lax.optimization_barrier(
        (shared_term.astype(jnp.bfloat16), normed_full)
    )
    shared_out = lax.psum_scatter(shared_term, "tensor", scatter_dimension=1, tiled=True)
    cap = tensor_count * (
        (4 * tok_dev * topk + 3 * experts * tensor_count - 1) // (3 * experts * tensor_count)
    )
    flat_ids = expert_ids.reshape(-1)
    marks = (flat_ids[:, None] == lax.iota(jnp.int32, experts)[None, :]).astype(jnp.int32)
    earlier = jnp.cumsum(marks, 0) - marks
    rank = jnp.sum(earlier * marks, 1)
    slot_index = flat_ids * cap + rank
    source_rows = (
        jnp.full((experts * cap,), tok_dev, jnp.int32)
        .at[slot_index]
        .set(lax.iota(jnp.int32, flat_ids.shape[0]) // topk)
    )
    padded_full = jnp.concatenate([normed_full, jnp.zeros((1, D), jnp.bfloat16)], 0)
    outgoing = padded_full[source_rows].reshape(seq_count, exp_dev, cap, D)
    routed_rows = lax.all_to_all(outgoing, "seq", split_axis=0, concat_axis=0, tiled=True)
    routed_rows, shared_out = lax.optimization_barrier((routed_rows, shared_out))
    expert_pair = jnp.einsum(
        "secd,edjf->secjf", routed_rows, expert_gate_up, preferred_element_type=jnp.float32
    )
    expert_act = (jax.nn.silu(expert_pair[..., 0, :]) * expert_pair[..., 1, :]).astype(jnp.bfloat16)
    expert_term = jnp.einsum(
        "secf,efd->secd", expert_act, expert_down, preferred_element_type=jnp.float32
    )
    expert_total = lax.psum_scatter(
        expert_term.astype(jnp.bfloat16), "tensor", scatter_dimension=3, tiled=True
    )
    returned = lax.all_to_all(expert_total, "seq", split_axis=0, concat_axis=0, tiled=True)
    picked = returned.reshape(experts * cap, width_local)[slot_index].reshape(
        tok_dev, topk, width_local
    )
    mixture = jnp.sum(gates[..., None] * picked.astype(jnp.float32), 1)
    return (stream + shared_out.astype(jnp.float32) + mixture).astype(jnp.bfloat16)


def solution(mesh):
    in_specs = (
        P("seq", "tensor"),
        P("seq", "tensor"),
        P("seq", "tensor"),
        P("seq", "tensor"),
        P(None, "seq", "tensor"),
        P(None, "seq", "tensor"),
        P(),
        P("tensor", None),
        P("tensor"),
        P("tensor", None),
        P("seq", None),
        P("seq", None, None, "tensor"),
        P("seq", "tensor", None),
        P(None, None, "tensor"),
        P("tensor", None),
    )
    out_specs = P("seq", "tensor")
    return jax.shard_map(shards, mesh=mesh, in_specs=in_specs, out_specs=out_specs, check_vma=False)
```

```python
import math

import jax
import jax.numpy as jnp
from jax import lax
from jax.sharding import PartitionSpec as P

D = 2048
HD = 128
NEW = 512


negative = -1e30
epsilon = 1e-06


def block_partial(scores, visible, values):
    masked = jnp.where(visible, scores, negative)
    block_max = jnp.max(masked, -1)
    shifted = jnp.where(visible, scores, block_max[..., None]) - block_max[..., None]
    weights = jnp.where(visible, jnp.exp(shifted), 0.0)
    block_sum = jnp.sum(weights, -1)
    block_out = jnp.einsum(
        "hqk,khd->qhd", weights.astype(jnp.bfloat16), values, preferred_element_type=jnp.float32
    )
    return (block_max, block_sum, block_out)


def shards(
    residual,
    queries,
    new_keys,
    new_values,
    cache_keys,
    cache_values,
    cache_lengths,
    out_proj,
    norm_gain,
    router,
    expert_ids,
    expert_gate_up,
    expert_down,
    shared_gate_up,
    shared_down,
):
    seq_count = lax.axis_size("seq")
    tensor_count = lax.axis_size("tensor")
    seq_index = lax.axis_index("seq")
    tok_dev = queries.shape[0]
    heads_local = queries.shape[1] // HD
    requests = tok_dev * seq_count // NEW
    clen_dev = cache_keys.shape[1]
    tokens = tok_dev * seq_count
    width_local = residual.shape[1]
    experts = router.shape[1]
    exp_dev = expert_gate_up.shape[0]
    topk = expert_ids.shape[1]
    scaling = 1.0 / math.sqrt(HD)
    first_place = seq_index * clen_dev
    own_start = seq_index * tok_dev
    own_request = own_start // NEW
    offset = own_start % NEW

    def attend(head):
        own = queries.reshape(tok_dev, heads_local, HD)[:, head : head + 1]
        spread = jnp.broadcast_to(own[None], (seq_count,) + own.shape)
        grouped = lax.all_to_all(spread, "seq", 0, 0, tiled=True).reshape(requests, NEW, 1, HD)
        keys = cache_keys.reshape(requests, clen_dev, heads_local, HD)[:, :, head : head + 1]
        values = cache_values.reshape(requests, clen_dev, heads_local, HD)[:, :, head : head + 1]
        cached_scores = (
            jnp.einsum("rqhd,rkhd->rhqk", grouped, keys, preferred_element_type=jnp.float32)
            * scaling
        )
        cached_visible = (
            first_place + lax.iota(jnp.int32, clen_dev)[None, :] < cache_lengths[:, None]
        )[:, None, None, :]
        masked = jnp.where(cached_visible, cached_scores, negative)
        max_cached = jnp.max(masked, -1)
        cached_weights = jnp.where(
            cached_visible, jnp.exp(cached_scores - max_cached[..., None]), 0.0
        )
        sum_cached = jnp.sum(cached_weights, -1)
        out_cached = jnp.einsum(
            "rhqk,rkhd->rqhd",
            cached_weights.astype(jnp.bfloat16),
            values,
            preferred_element_type=jnp.float32,
        )
        max_cached = jnp.transpose(max_cached, (0, 2, 1))
        sum_cached = jnp.transpose(sum_cached, (0, 2, 1))
        own_queries = lax.dynamic_index_in_dim(grouped, own_request, 0, keepdims=False)
        new_scores = (
            jnp.einsum(
                "qhd,khd->hqk",
                own_queries,
                new_keys.reshape(tok_dev, heads_local, HD)[:, head : head + 1],
                preferred_element_type=jnp.float32,
            )
            * scaling
        )
        visible_new = (
            lax.iota(jnp.int32, NEW)[:, None] >= offset + lax.iota(jnp.int32, tok_dev)[None, :]
        )[None]
        max_new, sum_new, out_new = block_partial(
            new_scores,
            visible_new,
            new_values.reshape(tok_dev, heads_local, HD)[:, head : head + 1],
        )
        chosen_request = (lax.iota(jnp.int32, requests) == own_request)[:, None, None]
        max_placed = jnp.where(chosen_request, jnp.transpose(max_new)[None], negative)
        sum_placed = jnp.where(chosen_request, jnp.transpose(sum_new)[None], 0.0)
        out_placed = jnp.where(chosen_request[..., None], out_new[None], 0.0)
        local_max = jnp.maximum(max_cached, max_placed)
        factor_cached = jnp.exp(max_cached - local_max)
        factor_new = jnp.exp(max_placed - local_max)
        local_sum = sum_cached * factor_cached + sum_placed * factor_new
        local_out = out_cached * factor_cached[..., None] + out_placed * factor_new[..., None]
        stats = lax.all_to_all(
            jnp.stack([local_max, local_sum], -1).reshape(seq_count, tok_dev, 2),
            "seq",
            0,
            0,
            tiled=True,
        )
        parts_out = lax.all_to_all(
            local_out.reshape(seq_count, tok_dev, HD).astype(jnp.bfloat16),
            "seq",
            0,
            0,
            tiled=True,
        ).astype(jnp.float32)
        part_max = stats[..., 0]
        row_max = jnp.max(part_max, 0)
        factors = jnp.exp(part_max - row_max[None])
        row_sum = jnp.sum(stats[..., 1] * factors, 0)
        weighted = jnp.sum(parts_out * factors[..., None], 0)
        return (weighted / row_sum[..., None]).astype(jnp.bfloat16)

    attended = jnp.concatenate([attend(head) for head in range(heads_local)], 1)
    projected = jnp.dot(attended, out_proj, preferred_element_type=jnp.float32)
    attn_out = lax.psum_scatter(
        projected.astype(jnp.bfloat16), "tensor", scatter_dimension=1, tiled=True
    ).astype(jnp.float32)
    stream = residual.astype(jnp.float32) + attn_out
    gathered = lax.all_gather(
        jnp.concatenate([stream, norm_gain[None], router.astype(jnp.float32).T], 0),
        "tensor",
        axis=1,
        tiled=True,
    )
    stream_full = gathered[:tok_dev]
    gain_full = gathered[tok_dev]
    router_full = gathered[tok_dev + 1 :].T.astype(jnp.bfloat16)
    inverse_rms = lax.rsqrt(jnp.sum(stream_full * stream_full, 1) / D + epsilon)
    normed_full = (stream_full * inverse_rms[:, None] * gain_full).astype(jnp.bfloat16)
    logits = jnp.dot(normed_full, router_full, preferred_element_type=jnp.float32)
    matches = expert_ids[:, :, None] == lax.iota(jnp.int32, experts)[None, None, :]
    selected = jnp.sum(jnp.where(matches, logits[:, None, :], 0.0), 2)
    sigmoids = jax.nn.sigmoid(selected)
    gates = sigmoids / jnp.sum(sigmoids, 1, keepdims=True)
    shared_pair = jnp.einsum(
        "td,dcf->tcf", normed_full, shared_gate_up, preferred_element_type=jnp.float32
    )
    shared_act = (jax.nn.silu(shared_pair[:, 0]) * shared_pair[:, 1]).astype(jnp.bfloat16)
    shared_term = jnp.dot(shared_act, shared_down, preferred_element_type=jnp.float32)
    shared_term, normed_full = lax.optimization_barrier(
        (shared_term.astype(jnp.bfloat16), normed_full)
    )
    shared_out = lax.psum_scatter(shared_term, "tensor", scatter_dimension=1, tiled=True)
    cap = tensor_count * (
        (4 * tok_dev * topk + 3 * experts * tensor_count - 1) // (3 * experts * tensor_count)
    )
    flat_ids = expert_ids.reshape(-1)
    marks = (flat_ids[:, None] == lax.iota(jnp.int32, experts)[None, :]).astype(jnp.int32)
    earlier = jnp.cumsum(marks, 0) - marks
    rank = jnp.sum(earlier * marks, 1)
    slot_index = flat_ids * cap + rank
    source_rows = (
        jnp.full((experts * cap,), tok_dev, jnp.int32)
        .at[slot_index]
        .set(lax.iota(jnp.int32, flat_ids.shape[0]) // topk)
    )
    padded_full = jnp.concatenate([normed_full, jnp.zeros((1, D), jnp.bfloat16)], 0)
    outgoing = padded_full[source_rows].reshape(seq_count, exp_dev, cap, D)
    routed_rows = lax.all_to_all(outgoing, "seq", split_axis=0, concat_axis=0, tiled=True)
    routed_rows, shared_out = lax.optimization_barrier((routed_rows, shared_out))
    expert_pair = jnp.einsum(
        "secd,edjf->secjf", routed_rows, expert_gate_up, preferred_element_type=jnp.float32
    )
    expert_act = (jax.nn.silu(expert_pair[..., 0, :]) * expert_pair[..., 1, :]).astype(jnp.bfloat16)
    expert_term = jnp.einsum(
        "secf,efd->secd", expert_act, expert_down, preferred_element_type=jnp.float32
    )
    expert_total = lax.psum_scatter(
        expert_term.astype(jnp.bfloat16), "tensor", scatter_dimension=3, tiled=True
    )
    returned = lax.all_to_all(expert_total, "seq", split_axis=0, concat_axis=0, tiled=True)
    picked = returned.reshape(experts * cap, width_local)[slot_index].reshape(
        tok_dev, topk, width_local
    )
    mixture = jnp.sum(gates[..., None] * picked.astype(jnp.float32), 1)
    return (stream + shared_out.astype(jnp.float32) + mixture).astype(jnp.bfloat16)


def solution(mesh):
    in_specs = (
        P("seq", "tensor"),
        P("seq", "tensor"),
        P("seq", "tensor"),
        P("seq", "tensor"),
        P(None, "seq", "tensor"),
        P(None, "seq", "tensor"),
        P(),
        P("tensor", None),
        P("tensor"),
        P("tensor", None),
        P("seq", None),
        P("seq", None, None, "tensor"),
        P("seq", "tensor", None),
        P(None, None, "tensor"),
        P("tensor", None),
    )
    out_specs = P("seq", "tensor")
    return jax.shard_map(shards, mesh=mesh, in_specs=in_specs, out_specs=out_specs, check_vma=False)
```

```python
import math

import jax
import jax.numpy as jnp
from jax import lax
from jax.sharding import PartitionSpec as P

D = 2048
HD = 128
NEW = 512


negative = -1e30
epsilon = 1e-06


def block_partial(scores, visible, values):
    masked = jnp.where(visible, scores, negative)
    block_max = jnp.max(masked, -1)
    shifted = jnp.where(visible, scores, block_max[..., None]) - block_max[..., None]
    weights = jnp.where(visible, jnp.exp(shifted), 0.0)
    block_sum = jnp.sum(weights, -1)
    block_out = jnp.einsum(
        "hqk,khd->qhd", weights.astype(jnp.bfloat16), values, preferred_element_type=jnp.float32
    )
    return (block_max, block_sum, block_out)


def shards(
    residual,
    queries,
    new_keys,
    new_values,
    cache_keys,
    cache_values,
    cache_lengths,
    out_proj,
    norm_gain,
    router,
    expert_ids,
    expert_gate_up,
    expert_down,
    shared_gate_up,
    shared_down,
):
    seq_count = lax.axis_size("seq")
    tensor_count = lax.axis_size("tensor")
    seq_index = lax.axis_index("seq")
    tok_dev = queries.shape[0]
    heads_local = queries.shape[1] // HD
    requests = tok_dev * seq_count // NEW
    clen_dev = cache_keys.shape[1]
    tokens = tok_dev * seq_count
    width_local = residual.shape[1]
    experts = router.shape[1]
    exp_dev = expert_gate_up.shape[0]
    topk = expert_ids.shape[1]
    scaling = 1.0 / math.sqrt(HD)
    spread = jnp.broadcast_to(queries[None], (seq_count,) + queries.shape)
    every_query = lax.all_to_all(spread, "seq", 0, 0, tiled=True).reshape(tokens, width_local)
    grouped = every_query.reshape(requests, NEW, heads_local, HD)
    first_place = seq_index * clen_dev

    cached_scores = (
        jnp.einsum(
            "rqhd,rkhd->rhqk",
            grouped,
            cache_keys.reshape(requests, clen_dev, heads_local, HD),
            preferred_element_type=jnp.float32,
        )
        * scaling
    )
    cached_visible = (
        first_place + lax.iota(jnp.int32, clen_dev)[None, :] < cache_lengths[:, None]
    )[:, None, None, :]
    masked = jnp.where(cached_visible, cached_scores, negative)
    max_cached = jnp.max(masked, -1)
    cached_weights = jnp.where(
        cached_visible, jnp.exp(cached_scores - max_cached[..., None]), 0.0
    )
    sum_cached = jnp.sum(cached_weights, -1)
    out_cached = jnp.einsum(
        "rhqk,rkhd->rqhd",
        cached_weights.astype(jnp.bfloat16),
        cache_values.reshape(requests, clen_dev, heads_local, HD),
        preferred_element_type=jnp.float32,
    )
    max_cached = jnp.transpose(max_cached, (0, 2, 1))
    sum_cached = jnp.transpose(sum_cached, (0, 2, 1))
    own_start = seq_index * tok_dev
    own_request = own_start // NEW
    offset = own_start % NEW
    own_queries = lax.dynamic_index_in_dim(grouped, own_request, 0, keepdims=False)
    new_scores = (
        jnp.einsum(
            "qhd,khd->hqk",
            own_queries,
            new_keys.reshape(tok_dev, heads_local, HD),
            preferred_element_type=jnp.float32,
        )
        * scaling
    )
    visible_new = (
        lax.iota(jnp.int32, NEW)[:, None] >= offset + lax.iota(jnp.int32, tok_dev)[None, :]
    )[None]
    max_new, sum_new, out_new = block_partial(
        new_scores, visible_new, new_values.reshape(tok_dev, heads_local, HD)
    )
    chosen_request = (lax.iota(jnp.int32, requests) == own_request)[:, None, None]
    max_placed = jnp.where(chosen_request, jnp.transpose(max_new)[None], negative)
    sum_placed = jnp.where(chosen_request, jnp.transpose(sum_new)[None], 0.0)
    out_placed = jnp.where(chosen_request[..., None], out_new[None], 0.0)
    local_max = jnp.maximum(max_cached, max_placed)
    factor_cached = jnp.exp(max_cached - local_max)
    factor_new = jnp.exp(max_placed - local_max)
    local_sum = sum_cached * factor_cached + sum_placed * factor_new
    local_out = out_cached * factor_cached[..., None] + out_placed * factor_new[..., None]
    flat_max = local_max.reshape(seq_count, tok_dev, heads_local)
    flat_sum = local_sum.reshape(seq_count, tok_dev, heads_local)
    stats = lax.all_to_all(
        jnp.stack([flat_max, flat_sum], -1), "seq", 0, 0, tiled=True
    )
    parts_out = lax.all_to_all(
        local_out.reshape(seq_count, tok_dev, heads_local, HD).astype(jnp.bfloat16),
        "seq",
        0,
        0,
        tiled=True,
    ).astype(jnp.float32)
    part_max = stats[..., 0]
    row_max = jnp.max(part_max, 0)
    factors = jnp.exp(part_max - row_max[None])
    row_sum = jnp.sum(stats[..., 1] * factors, 0)
    weighted = jnp.sum(parts_out * factors[..., None], 0)
    attended = (
        (weighted / row_sum[..., None]).astype(jnp.bfloat16).reshape(tok_dev, heads_local * HD)
    )
    projected = jnp.dot(attended, out_proj, preferred_element_type=jnp.float32)
    attn_out = lax.psum_scatter(
        projected.astype(jnp.bfloat16), "tensor", scatter_dimension=1, tiled=True
    ).astype(jnp.float32)
    stream = residual.astype(jnp.float32) + attn_out
    gathered = lax.all_gather(
        jnp.concatenate([stream, norm_gain[None], router.astype(jnp.float32).T], 0),
        "tensor",
        axis=1,
        tiled=True,
    )
    stream_full = gathered[:tok_dev]
    gain_full = gathered[tok_dev]
    router_full = gathered[tok_dev + 1 :].T.astype(jnp.bfloat16)
    inverse_rms = lax.rsqrt(jnp.sum(stream_full * stream_full, 1) / D + epsilon)
    normed_full = (stream_full * inverse_rms[:, None] * gain_full).astype(jnp.bfloat16)
    logits = jnp.dot(normed_full, router_full, preferred_element_type=jnp.float32)
    matches = expert_ids[:, :, None] == lax.iota(jnp.int32, experts)[None, None, :]
    selected = jnp.sum(jnp.where(matches, logits[:, None, :], 0.0), 2)
    sigmoids = jax.nn.sigmoid(selected)
    gates = sigmoids / jnp.sum(sigmoids, 1, keepdims=True)
    shared_pair = jnp.einsum(
        "td,dcf->tcf", normed_full, shared_gate_up, preferred_element_type=jnp.float32
    )
    shared_act = (jax.nn.silu(shared_pair[:, 0]) * shared_pair[:, 1]).astype(jnp.bfloat16)
    shared_term = jnp.dot(shared_act, shared_down, preferred_element_type=jnp.float32)
    cap = tensor_count * (
        (4 * tok_dev * topk + 3 * experts * tensor_count - 1) // (3 * experts * tensor_count)
    )
    flat_ids = expert_ids.reshape(-1)
    marks = (flat_ids[:, None] == lax.iota(jnp.int32, experts)[None, :]).astype(jnp.int32)
    earlier = jnp.cumsum(marks, 0) - marks
    rank = jnp.sum(earlier * marks, 1)
    slot_index = flat_ids * cap + rank
    source_rows = (
        jnp.full((experts * cap,), tok_dev, jnp.int32)
        .at[slot_index]
        .set(lax.iota(jnp.int32, flat_ids.shape[0]) // topk)
    )
    padded_full = jnp.concatenate([normed_full, jnp.zeros((1, D), jnp.bfloat16)], 0)
    outgoing = padded_full[source_rows].reshape(seq_count, exp_dev, cap, D)
    routed_rows = lax.all_to_all(outgoing, "seq", split_axis=0, concat_axis=0, tiled=True)
    expert_pair = jnp.einsum(
        "secd,edjf->secjf", routed_rows, expert_gate_up, preferred_element_type=jnp.float32
    )
    expert_act = (jax.nn.silu(expert_pair[..., 0, :]) * expert_pair[..., 1, :]).astype(jnp.bfloat16)
    expert_term = jnp.einsum(
        "secf,efd->secd", expert_act, expert_down, preferred_element_type=jnp.float32
    )
    expert_rows = seq_count * exp_dev * cap
    summed = lax.psum_scatter(
        jnp.concatenate(
            [
                expert_term.astype(jnp.bfloat16).reshape(expert_rows, D),
                shared_term.astype(jnp.bfloat16),
            ],
            0,
        ),
        "tensor",
        scatter_dimension=1,
        tiled=True,
    )
    expert_total = summed[:expert_rows].reshape(seq_count, exp_dev, cap, width_local)
    shared_out = summed[expert_rows:]
    returned = lax.all_to_all(expert_total, "seq", split_axis=0, concat_axis=0, tiled=True)
    picked = returned.reshape(experts * cap, width_local)[slot_index].reshape(
        tok_dev, topk, width_local
    )
    mixture = jnp.sum(gates[..., None] * picked.astype(jnp.float32), 1)
    return (stream + shared_out.astype(jnp.float32) + mixture).astype(jnp.bfloat16)


def solution(mesh):
    in_specs = (
        P("seq", "tensor"),
        P("seq", "tensor"),
        P("seq", "tensor"),
        P("seq", "tensor"),
        P(None, "seq", "tensor"),
        P(None, "seq", "tensor"),
        P(),
        P("tensor", None),
        P("tensor"),
        P("tensor", None),
        P("seq", None),
        P("seq", None, None, "tensor"),
        P("seq", "tensor", None),
        P(None, None, "tensor"),
        P("tensor", None),
    )
    out_specs = P("seq", "tensor")
    return jax.shard_map(shards, mesh=mesh, in_specs=in_specs, out_specs=out_specs, check_vma=False)
```

```python
import math

import jax
import jax.numpy as jnp
from jax import lax
from jax.sharding import PartitionSpec as P

D = 2048
HD = 128
NEW = 512


negative = -1e30
epsilon = 1e-06


def block_partial(scores, visible, values):
    masked = jnp.where(visible, scores, negative)
    block_max = jnp.max(masked, -1)
    shifted = jnp.where(visible, scores, block_max[..., None]) - block_max[..., None]
    weights = jnp.where(visible, jnp.exp(shifted), 0.0)
    block_sum = jnp.sum(weights, -1)
    block_out = jnp.einsum(
        "hqk,khd->qhd", weights.astype(jnp.bfloat16), values, preferred_element_type=jnp.float32
    )
    return (block_max, block_sum, block_out)


def shards(
    residual,
    queries,
    new_keys,
    new_values,
    cache_keys,
    cache_values,
    cache_lengths,
    out_proj,
    norm_gain,
    router,
    expert_ids,
    expert_gate_up,
    expert_down,
    shared_gate_up,
    shared_down,
):
    seq_count = lax.axis_size("seq")
    tensor_count = lax.axis_size("tensor")
    seq_index = lax.axis_index("seq")
    tok_dev = queries.shape[0]
    heads_local = queries.shape[1] // HD
    requests = tok_dev * seq_count // NEW
    clen_dev = cache_keys.shape[1]
    tokens = tok_dev * seq_count
    width_local = residual.shape[1]
    experts = router.shape[1]
    exp_dev = expert_gate_up.shape[0]
    topk = expert_ids.shape[1]
    scaling = 1.0 / math.sqrt(HD)
    spread = jnp.broadcast_to(queries[None], (seq_count,) + queries.shape)
    every_query = lax.all_to_all(spread, "seq", 0, 0, tiled=True).reshape(tokens, width_local)
    grouped = every_query.reshape(requests, NEW, heads_local, HD)
    first_place = seq_index * clen_dev

    cached_scores = (
        jnp.einsum(
            "rqhd,rkhd->rhqk",
            grouped,
            cache_keys.reshape(requests, clen_dev, heads_local, HD),
            preferred_element_type=jnp.float32,
        )
        * scaling
    )
    cached_visible = (
        first_place + lax.iota(jnp.int32, clen_dev)[None, :] < cache_lengths[:, None]
    )[:, None, None, :]
    masked = jnp.where(cached_visible, cached_scores, negative)
    max_cached = jnp.max(masked, -1)
    cached_weights = jnp.where(
        cached_visible, jnp.exp(cached_scores - max_cached[..., None]), 0.0
    )
    sum_cached = jnp.sum(cached_weights, -1)
    out_cached = jnp.einsum(
        "rhqk,rkhd->rqhd",
        cached_weights.astype(jnp.bfloat16),
        cache_values.reshape(requests, clen_dev, heads_local, HD),
        preferred_element_type=jnp.float32,
    )
    max_cached = jnp.transpose(max_cached, (0, 2, 1))
    sum_cached = jnp.transpose(sum_cached, (0, 2, 1))
    own_start = seq_index * tok_dev
    own_request = own_start // NEW
    offset = own_start % NEW
    own_queries = lax.dynamic_index_in_dim(grouped, own_request, 0, keepdims=False)
    new_scores = (
        jnp.einsum(
            "qhd,khd->hqk",
            own_queries,
            new_keys.reshape(tok_dev, heads_local, HD),
            preferred_element_type=jnp.float32,
        )
        * scaling
    )
    visible_new = (
        lax.iota(jnp.int32, NEW)[:, None] >= offset + lax.iota(jnp.int32, tok_dev)[None, :]
    )[None]
    max_new, sum_new, out_new = block_partial(
        new_scores, visible_new, new_values.reshape(tok_dev, heads_local, HD)
    )
    chosen_request = (lax.iota(jnp.int32, requests) == own_request)[:, None, None]
    max_placed = jnp.where(chosen_request, jnp.transpose(max_new)[None], negative)
    sum_placed = jnp.where(chosen_request, jnp.transpose(sum_new)[None], 0.0)
    out_placed = jnp.where(chosen_request[..., None], out_new[None], 0.0)
    local_max = jnp.maximum(max_cached, max_placed)
    factor_cached = jnp.exp(max_cached - local_max)
    factor_new = jnp.exp(max_placed - local_max)
    local_sum = sum_cached * factor_cached + sum_placed * factor_new
    local_out = out_cached * factor_cached[..., None] + out_placed * factor_new[..., None]
    flat_max = local_max.reshape(seq_count, tok_dev, heads_local)
    flat_sum = local_sum.reshape(seq_count, tok_dev, heads_local)
    stats = lax.all_to_all(
        jnp.stack([flat_max, flat_sum], -1), "seq", 0, 0, tiled=True
    )
    parts_out = lax.all_to_all(
        local_out.reshape(seq_count, tok_dev, heads_local, HD).astype(jnp.bfloat16),
        "seq",
        0,
        0,
        tiled=True,
    ).astype(jnp.float32)
    part_max = stats[..., 0]
    row_max = jnp.max(part_max, 0)
    factors = jnp.exp(part_max - row_max[None])
    row_sum = jnp.sum(stats[..., 1] * factors, 0)
    weighted = jnp.sum(parts_out * factors[..., None], 0)
    attended = (
        (weighted / row_sum[..., None]).astype(jnp.bfloat16).reshape(tok_dev, heads_local * HD)
    )
    projected = jnp.dot(attended, out_proj, preferred_element_type=jnp.float32)
    attn_parts = lax.all_to_all(
        jnp.transpose(
            projected.astype(jnp.bfloat16).reshape(tok_dev, tensor_count, width_local), (1, 0, 2)
        ),
        "tensor",
        0,
        0,
        tiled=True,
    )
    attn_out = jnp.sum(attn_parts.astype(jnp.float32), 0)
    stream = residual.astype(jnp.float32) + attn_out
    gathered = lax.all_gather(
        jnp.concatenate([stream, norm_gain[None], router.astype(jnp.float32).T], 0),
        "tensor",
        axis=1,
        tiled=True,
    )
    stream_full = gathered[:tok_dev]
    gain_full = gathered[tok_dev]
    router_full = gathered[tok_dev + 1 :].T.astype(jnp.bfloat16)
    inverse_rms = lax.rsqrt(jnp.sum(stream_full * stream_full, 1) / D + epsilon)
    normed_full = (stream_full * inverse_rms[:, None] * gain_full).astype(jnp.bfloat16)
    logits = jnp.dot(normed_full, router_full, preferred_element_type=jnp.float32)
    matches = expert_ids[:, :, None] == lax.iota(jnp.int32, experts)[None, None, :]
    selected = jnp.sum(jnp.where(matches, logits[:, None, :], 0.0), 2)
    sigmoids = jax.nn.sigmoid(selected)
    gates = sigmoids / jnp.sum(sigmoids, 1, keepdims=True)
    shared_pair = jnp.einsum(
        "td,dcf->tcf", normed_full, shared_gate_up, preferred_element_type=jnp.float32
    )
    shared_act = (jax.nn.silu(shared_pair[:, 0]) * shared_pair[:, 1]).astype(jnp.bfloat16)
    shared_term = jnp.dot(shared_act, shared_down, preferred_element_type=jnp.float32)
    shared_term, normed_full = lax.optimization_barrier(
        (shared_term.astype(jnp.bfloat16), normed_full)
    )
    shared_out = lax.psum_scatter(shared_term, "tensor", scatter_dimension=1, tiled=True)
    cap = tensor_count * (
        (4 * tok_dev * topk + 3 * experts * tensor_count - 1) // (3 * experts * tensor_count)
    )
    flat_ids = expert_ids.reshape(-1)
    marks = (flat_ids[:, None] == lax.iota(jnp.int32, experts)[None, :]).astype(jnp.int32)
    earlier = jnp.cumsum(marks, 0) - marks
    rank = jnp.sum(earlier * marks, 1)
    slot_index = flat_ids * cap + rank
    source_rows = (
        jnp.full((experts * cap,), tok_dev, jnp.int32)
        .at[slot_index]
        .set(lax.iota(jnp.int32, flat_ids.shape[0]) // topk)
    )
    padded_full = jnp.concatenate([normed_full, jnp.zeros((1, D), jnp.bfloat16)], 0)
    outgoing = padded_full[source_rows].reshape(seq_count, exp_dev, cap, D)
    routed_rows = lax.all_to_all(outgoing, "seq", split_axis=0, concat_axis=0, tiled=True)
    routed_rows, shared_out = lax.optimization_barrier((routed_rows, shared_out))
    expert_pair = jnp.einsum(
        "secd,edjf->secjf", routed_rows, expert_gate_up, preferred_element_type=jnp.float32
    )
    expert_act = (jax.nn.silu(expert_pair[..., 0, :]) * expert_pair[..., 1, :]).astype(jnp.bfloat16)
    expert_term = jnp.einsum(
        "secf,efd->secd", expert_act, expert_down, preferred_element_type=jnp.float32
    )
    expert_total = lax.psum_scatter(
        expert_term.astype(jnp.bfloat16), "tensor", scatter_dimension=3, tiled=True
    )
    returned = lax.all_to_all(expert_total, "seq", split_axis=0, concat_axis=0, tiled=True)
    picked = returned.reshape(experts * cap, width_local)[slot_index].reshape(
        tok_dev, topk, width_local
    )
    mixture = jnp.sum(gates[..., None] * picked.astype(jnp.float32), 1)
    return (stream + shared_out.astype(jnp.float32) + mixture).astype(jnp.bfloat16)


def solution(mesh):
    in_specs = (
        P("seq", "tensor"),
        P("seq", "tensor"),
        P("seq", "tensor"),
        P("seq", "tensor"),
        P(None, "seq", "tensor"),
        P(None, "seq", "tensor"),
        P(),
        P("tensor", None),
        P("tensor"),
        P("tensor", None),
        P("seq", None),
        P("seq", None, None, "tensor"),
        P("seq", "tensor", None),
        P(None, None, "tensor"),
        P("tensor", None),
    )
    out_specs = P("seq", "tensor")
    return jax.shard_map(shards, mesh=mesh, in_specs=in_specs, out_specs=out_specs, check_vma=False)
```

```python
import math

import jax
import jax.numpy as jnp
from jax import lax
from jax.sharding import PartitionSpec as P

D = 2048
HD = 128
NEW = 512


negative = -1e30
epsilon = 1e-06


def block_partial(scores, visible, values):
    masked = jnp.where(visible, scores, negative)
    block_max = jnp.max(masked, -1)
    shifted = jnp.where(visible, scores, block_max[..., None]) - block_max[..., None]
    weights = jnp.where(visible, jnp.exp(shifted), 0.0)
    block_sum = jnp.sum(weights, -1)
    block_out = jnp.einsum(
        "hqk,khd->qhd", weights.astype(jnp.bfloat16), values, preferred_element_type=jnp.float32
    )
    return (block_max, block_sum, block_out)


def shards(
    residual,
    queries,
    new_keys,
    new_values,
    cache_keys,
    cache_values,
    cache_lengths,
    out_proj,
    norm_gain,
    router,
    expert_ids,
    expert_gate_up,
    expert_down,
    shared_gate_up,
    shared_down,
):
    seq_count = lax.axis_size("seq")
    tensor_count = lax.axis_size("tensor")
    seq_index = lax.axis_index("seq")
    tok_dev = queries.shape[0]
    heads_local = queries.shape[1] // HD
    requests = tok_dev * seq_count // NEW
    clen_dev = cache_keys.shape[1]
    tokens = tok_dev * seq_count
    width_local = residual.shape[1]
    experts = router.shape[1]
    exp_dev = expert_gate_up.shape[0]
    topk = expert_ids.shape[1]
    scaling = 1.0 / math.sqrt(HD)
    spread = jnp.broadcast_to(queries[None], (seq_count,) + queries.shape)
    every_query = lax.all_to_all(spread, "seq", 0, 0, tiled=True).reshape(tokens, width_local)
    grouped = every_query.reshape(requests, NEW, heads_local, HD)
    first_place = seq_index * clen_dev

    cached_scores = (
        jnp.einsum(
            "rqhd,rkhd->rhqk",
            grouped,
            cache_keys.reshape(requests, clen_dev, heads_local, HD),
            preferred_element_type=jnp.float32,
        )
        * scaling
    )
    cached_visible = (
        first_place + lax.iota(jnp.int32, clen_dev)[None, :] < cache_lengths[:, None]
    )[:, None, None, :]
    masked = jnp.where(cached_visible, cached_scores, negative)
    max_cached = jnp.max(masked, -1)
    cached_weights = jnp.where(
        cached_visible, jnp.exp(cached_scores - max_cached[..., None]), 0.0
    )
    sum_cached = jnp.sum(cached_weights, -1)
    out_cached = jnp.einsum(
        "rhqk,rkhd->rqhd",
        cached_weights.astype(jnp.bfloat16),
        cache_values.reshape(requests, clen_dev, heads_local, HD),
        preferred_element_type=jnp.float32,
    )
    max_cached = jnp.transpose(max_cached, (0, 2, 1))
    sum_cached = jnp.transpose(sum_cached, (0, 2, 1))
    own_start = seq_index * tok_dev
    own_request = own_start // NEW
    offset = own_start % NEW
    own_queries = lax.dynamic_index_in_dim(grouped, own_request, 0, keepdims=False)
    new_scores = (
        jnp.einsum(
            "qhd,khd->hqk",
            own_queries,
            new_keys.reshape(tok_dev, heads_local, HD),
            preferred_element_type=jnp.float32,
        )
        * scaling
    )
    visible_new = (
        lax.iota(jnp.int32, NEW)[:, None] >= offset + lax.iota(jnp.int32, tok_dev)[None, :]
    )[None]
    max_new, sum_new, out_new = block_partial(
        new_scores, visible_new, new_values.reshape(tok_dev, heads_local, HD)
    )
    chosen_request = (lax.iota(jnp.int32, requests) == own_request)[:, None, None]
    max_placed = jnp.where(chosen_request, jnp.transpose(max_new)[None], negative)
    sum_placed = jnp.where(chosen_request, jnp.transpose(sum_new)[None], 0.0)
    out_placed = jnp.where(chosen_request[..., None], out_new[None], 0.0)
    local_max = jnp.maximum(max_cached, max_placed)
    factor_cached = jnp.exp(max_cached - local_max)
    factor_new = jnp.exp(max_placed - local_max)
    local_sum = sum_cached * factor_cached + sum_placed * factor_new
    local_out = out_cached * factor_cached[..., None] + out_placed * factor_new[..., None]
    flat_max = local_max.reshape(seq_count, tok_dev, heads_local)
    flat_sum = local_sum.reshape(seq_count, tok_dev, heads_local)
    stats = lax.all_to_all(
        jnp.stack([flat_max, flat_sum], -1), "seq", 0, 0, tiled=True
    )
    parts_out = lax.all_to_all(
        local_out.reshape(seq_count, tok_dev, heads_local, HD).astype(jnp.bfloat16),
        "seq",
        0,
        0,
        tiled=True,
    ).astype(jnp.float32)
    part_max = stats[..., 0]
    row_max = jnp.max(part_max, 0)
    factors = jnp.exp(part_max - row_max[None])
    row_sum = jnp.sum(stats[..., 1] * factors, 0)
    weighted = jnp.sum(parts_out * factors[..., None], 0)
    attended = (
        (weighted / row_sum[..., None]).astype(jnp.bfloat16).reshape(tok_dev, heads_local * HD)
    )
    projected = jnp.dot(attended, out_proj, preferred_element_type=jnp.float32)
    attn_parts = lax.all_to_all(
        jnp.transpose(
            projected.astype(jnp.bfloat16).reshape(tok_dev, tensor_count, width_local), (1, 0, 2)
        ),
        "tensor",
        0,
        0,
        tiled=True,
    )
    attn_out = jnp.sum(attn_parts.astype(jnp.float32), 0)
    stream = residual.astype(jnp.float32) + attn_out
    weights_full = lax.all_gather(
        jnp.concatenate([norm_gain[None], router.astype(jnp.float32).T], 0),
        "tensor",
        axis=1,
        tiled=True,
    )
    stream_full = lax.all_gather(stream, "tensor", axis=1, tiled=True)
    gain_full = weights_full[0]
    router_full = weights_full[1:].T.astype(jnp.bfloat16)
    inverse_rms = lax.rsqrt(jnp.sum(stream_full * stream_full, 1) / D + epsilon)
    normed_full = (stream_full * inverse_rms[:, None] * gain_full).astype(jnp.bfloat16)
    logits = jnp.dot(normed_full, router_full, preferred_element_type=jnp.float32)
    matches = expert_ids[:, :, None] == lax.iota(jnp.int32, experts)[None, None, :]
    selected = jnp.sum(jnp.where(matches, logits[:, None, :], 0.0), 2)
    sigmoids = jax.nn.sigmoid(selected)
    gates = sigmoids / jnp.sum(sigmoids, 1, keepdims=True)
    shared_pair = jnp.einsum(
        "td,dcf->tcf", normed_full, shared_gate_up, preferred_element_type=jnp.float32
    )
    shared_act = (jax.nn.silu(shared_pair[:, 0]) * shared_pair[:, 1]).astype(jnp.bfloat16)
    shared_term = jnp.dot(shared_act, shared_down, preferred_element_type=jnp.float32)
    shared_term, normed_full = lax.optimization_barrier(
        (shared_term.astype(jnp.bfloat16), normed_full)
    )
    shared_out = lax.psum_scatter(shared_term, "tensor", scatter_dimension=1, tiled=True)
    cap = tensor_count * (
        (4 * tok_dev * topk + 3 * experts * tensor_count - 1) // (3 * experts * tensor_count)
    )
    flat_ids = expert_ids.reshape(-1)
    marks = (flat_ids[:, None] == lax.iota(jnp.int32, experts)[None, :]).astype(jnp.int32)
    earlier = jnp.cumsum(marks, 0) - marks
    rank = jnp.sum(earlier * marks, 1)
    slot_index = flat_ids * cap + rank
    source_rows = (
        jnp.full((experts * cap,), tok_dev, jnp.int32)
        .at[slot_index]
        .set(lax.iota(jnp.int32, flat_ids.shape[0]) // topk)
    )
    padded_full = jnp.concatenate([normed_full, jnp.zeros((1, D), jnp.bfloat16)], 0)
    outgoing = padded_full[source_rows].reshape(seq_count, exp_dev, cap, D)
    routed_rows = lax.all_to_all(outgoing, "seq", split_axis=0, concat_axis=0, tiled=True)
    routed_rows, shared_out = lax.optimization_barrier((routed_rows, shared_out))
    expert_pair = jnp.einsum(
        "secd,edjf->secjf", routed_rows, expert_gate_up, preferred_element_type=jnp.float32
    )
    expert_act = (jax.nn.silu(expert_pair[..., 0, :]) * expert_pair[..., 1, :]).astype(jnp.bfloat16)
    expert_term = jnp.einsum(
        "secf,efd->secd", expert_act, expert_down, preferred_element_type=jnp.float32
    )
    expert_total = lax.psum_scatter(
        expert_term.astype(jnp.bfloat16), "tensor", scatter_dimension=3, tiled=True
    )
    returned = lax.all_to_all(expert_total, "seq", split_axis=0, concat_axis=0, tiled=True)
    picked = returned.reshape(experts * cap, width_local)[slot_index].reshape(
        tok_dev, topk, width_local
    )
    mixture = jnp.sum(gates[..., None] * picked.astype(jnp.float32), 1)
    return (stream + shared_out.astype(jnp.float32) + mixture).astype(jnp.bfloat16)


def solution(mesh):
    in_specs = (
        P("seq", "tensor"),
        P("seq", "tensor"),
        P("seq", "tensor"),
        P("seq", "tensor"),
        P(None, "seq", "tensor"),
        P(None, "seq", "tensor"),
        P(),
        P("tensor", None),
        P("tensor"),
        P("tensor", None),
        P("seq", None),
        P("seq", None, None, "tensor"),
        P("seq", "tensor", None),
        P(None, None, "tensor"),
        P("tensor", None),
    )
    out_specs = P("seq", "tensor")
    return jax.shard_map(shards, mesh=mesh, in_specs=in_specs, out_specs=out_specs, check_vma=False)
```
